256 devices in a mesh: sec: 2 (over z_lo), col: 128 (over z_hi, y, x, core).
Axes of the slice: x: 4, y: 4, z: 8 (z_hi: 4, z_lo: 2; z = z_hi * 2 + z_lo), core: 2. Of those that a mesh axis runs over, the one named last changes fastest.
Arguments:
- velocity: bfloat16 [2, 3, 1024, 128, 128], P('sec', None, None, 'col'), may hold values from -6 to 6
- thrust: float32 [128], replicated, may hold values from 1 to 8
- band_counts: int32 [2, 10], P('sec'), may hold values from 1 to 32, as said below
- farm_split: int32 [1], replicated, may hold values from 256 to 767
- turbine_cells: int32 [128, 3], replicated, may hold values from 0 to 1023, as said below
Outputs:
- velocity_next: bfloat16 [2, 3, 1024, 128, 128], P('sec', None, None, 'col')
- pressure: float32 [2, 1024, 128, 128], P('sec', None, 'col')
The draws below stay inside these ranges and needn't reach their ends.
Inputs may be any that keep to these rules, and one draw needn't show every extreme that they name: `band_counts`: band 0 of each section keeps all 32 modes. `turbine_cells`: column 0 is below 1024, column 1 below 128, column 2 from 16 to 63; cells may repeat.
All inputs are finite; a program needn't handle non-finite values.
Results may differ from the reference program's by a relative error of at most 0.0014.
The reference program's roundings to bfloat16 on the way count: a program that leaves them out, or rounds other values in their place, can miss the bound.
Values may be sent and summed in bfloat16 or wider, within the bound.
No kernel may reach another device: no remote copies, remote signals or barrier semaphores. Data moves between devices by JAX's collectives and lax.ppermute only.
A program may use at most 64 MiB of HBM per device.

```python
import math
import jax
import jax.numpy as jnp
from jax import lax

NX = 1024
NZ = 128
BAND = 32
NB = 10
FR = 32
NTURB = 128
DISK = 4
NY = 128
KX = 320


def draw_band_counts(key, part):
    counts = jax.random.randint(key, (2, NB), 1, BAND + 1, dtype=jnp.int32)
    return counts.at[:, 0].set(BAND)


def draw_turbine_cells(key, part):
    key_x = jax.random.fold_in(key, 11)
    key_y = jax.random.fold_in(key, 12)
    key_z = jax.random.fold_in(key, 13)
    cell_x = jax.random.randint(key_x, (NTURB,), 0, NX, dtype=jnp.int32)
    cell_y = jax.random.randint(key_y, (NTURB,), 0, NY, dtype=jnp.int32)
    cell_z = jax.random.randint(key_z, (NTURB,), NZ // 8, NZ // 2, dtype=jnp.int32)
    return jnp.stack([cell_x, cell_y, cell_z], axis=1)


def shard_levels(stream_key, extent, shards, low, high):
    gain, own = 1.0, jax.random.fold_in(stream_key, 6)
    for dim, blocks in shards:
        draws = jnp.exp(jax.random.uniform(jax.random.fold_in(own, dim), (blocks,), jnp.float32, low / len(shards), high / len(shards)))
        gain = gain * jnp.repeat(draws, extent[dim] // blocks).reshape([-1 if axis == dim else 1 for axis in range(len(extent))])
    return gain


def bell_draw(key, extent, deviation, bound, cuts=(), kind=jnp.bfloat16):
    entries = jax.random.normal(key, extent, jnp.float32) * deviation
    if len(cuts) > 0:
        entries = shard_levels(key, extent, cuts, -0.22, 0.18) * entries
    return jnp.clip(entries, min=-bound, max=bound).astype(kind)


def setup_inputs(seed: int = 0) -> dict:
    streams_of = jax.random.split(jax.random.key(seed), 6)
    return {
        "velocity": bell_draw(streams_of[0], (2, 3, NX, NY, NZ), 1.0, 6.0, ((0, 2), (3, 128))),
        "thrust": jnp.clip(jnp.exp(jax.random.uniform(streams_of[1], (NTURB,), jnp.float32, math.log(1.0), math.log(8.0))), 1.0, 8.0),
        "band_counts": draw_band_counts(jax.random.fold_in(streams_of[5], 71), 0),
        "farm_split": jax.random.randint(streams_of[3], (1,), NX // 4, 3 * NX // 4).astype(jnp.int32),
        "turbine_cells": draw_turbine_cells(jax.random.fold_in(streams_of[5], 71), 0),
    }


highest = lax.Precision.HIGHEST
time_step = 0.25
screen = 0.01
fringe_rate = 2.0

def spectral_diff(length):
    index = jnp.arange(length, dtype=jnp.int32)
    offset = (index[:, None] - index[None, :]) % length
    angle = jnp.pi * offset.astype(jnp.float32) / length
    parity = 1.0 - 2.0 * (offset % 2).astype(jnp.float32)
    denom = jnp.where(offset == 0, 1.0, jnp.sin(angle))
    return jnp.where(offset == 0, 0.0, 0.5 * parity * jnp.cos(angle) / denom).astype(jnp.float32)

def cas_matrix(mode_ids, length):
    cells = jnp.arange(length, dtype=jnp.int32)
    phase = mode_ids.astype(jnp.int32)[:, None] * cells[None, :] % length
    angle = 2.0 * jnp.pi * phase.astype(jnp.float32) / length
    return (jnp.cos(angle) + jnp.sin(angle)).astype(jnp.float32)

def cosine_table(length):
    index = jnp.arange(length, dtype=jnp.int32)
    phase = index[:, None] * (2 * index[None, :] + 1) % (4 * length)
    angle = jnp.pi * phase.astype(jnp.float32) / (2 * length)
    scale = jnp.where(index == 0, jnp.sqrt(1.0 / length), jnp.sqrt(2.0 / length)).astype(jnp.float32)
    return (jnp.cos(angle) * scale[:, None]).astype(jnp.float32)

def wave_square(mode_ids, length):
    folded = jnp.minimum(mode_ids, length - mode_ids).astype(jnp.float32)
    return (2.0 * jnp.pi * folded / length) ** 2

def signed_wave(length):
    index = jnp.arange(length, dtype=jnp.int32)
    signed = jnp.where(index < length // 2, index, jnp.where(index > length // 2, index - length, 0))
    return 2.0 * jnp.pi * signed.astype(jnp.float32) / length

def kept_mask(mode_ids, counts):
    folded = jnp.minimum(mode_ids, NX - mode_ids)
    band_of = folded // BAND
    onehot = band_of[:, None] == jnp.arange(NB, dtype=jnp.int32)[None, :]
    limit_per = lax.optimization_barrier(jnp.sum(jnp.where(onehot, counts[None, :], 0), axis=1))
    return ((folded < KX) & (folded % BAND < limit_per)).astype(jnp.float32)

def zdiff(field):
    zeros = jnp.zeros(field.shape[:-1] + (1,), jnp.float32)
    upper = jnp.concatenate([field[..., 1:], zeros], axis=-1)
    lower = jnp.concatenate([zeros, field[..., :-1]], axis=-1)
    return (upper - lower) * 0.5

def fringe_weights(split_at):
    cells = jnp.arange(NX, dtype=jnp.int32)[:, None]
    plane = jnp.arange(FR, dtype=jnp.int32)[None, :]
    rate = fringe_rate * jnp.sin(jnp.pi * (plane.astype(jnp.float32) + 0.5) / FR) ** 2
    inside = (cells == plane) | (cells == split_at + plane)
    return jnp.where(inside, rate, 0.0).astype(jnp.float32)

def turbine_field(cells, thrust, ycoord, count_z, span_total):
    onehot_x = (cells[:, 0][:, None] == jnp.arange(NX, dtype=jnp.int32)[None, :]).astype(jnp.float32) * thrust[:, None]
    offset_y = (ycoord[None, :] - cells[:, 1][:, None]) % span_total
    onehot_y = ((offset_y <= DISK) | (offset_y >= span_total - DISK)).astype(jnp.float32)
    offset_z = jnp.abs(jnp.arange(count_z, dtype=jnp.int32)[None, :] - cells[:, 2][:, None])
    onehot_z = (offset_z <= DISK).astype(jnp.float32)
    cross_yz = (onehot_y[:, :, None] * onehot_z[:, None, :]).reshape(cells.shape[0], -1)
    field = jnp.dot(onehot_x.T, cross_yz, precision=highest)
    return field.reshape(NX, ycoord.shape[0], count_z)

def column_solve(columns, local_modes):
    cells_y = columns.shape[1]
    cells_z = columns.shape[2]
    cas_y = cas_matrix(jnp.arange(cells_y, dtype=jnp.int32), cells_y)
    cos_z = cosine_table(cells_z)
    first = jnp.einsum('jy,ryz->rjz', cas_y, columns, precision=highest)
    second = jnp.einsum('rjz,mz->rjm', first, cos_z, precision=highest)
    kz_sq = (jnp.pi * jnp.arange(cells_z, dtype=jnp.int32).astype(jnp.float32) / cells_z) ** 2
    eigen = wave_square(local_modes, NX)[:, None, None] + wave_square(jnp.arange(cells_y, dtype=jnp.int32), cells_y)[None, :, None] + kz_sq[None, None, :] + screen
    p_hat = -second / eigen
    g_hat = -signed_wave(cells_y)[None, :, None] * jnp.roll(jnp.flip(p_hat, axis=1), 1, axis=1)

    def inverse(coeffs):
        back = jnp.einsum('jy,rjm->rym', cas_y, coeffs, precision=highest) / cells_y
        return jnp.einsum('rym,mz->ryz', back, cos_z, precision=highest)
    return (inverse(p_hat), inverse(g_hat))

def reference(velocity, thrust, band_counts, farm_split, turbine_cells):
    deriv_mat = spectral_diff(NX)
    deriv_bf = deriv_mat.astype(jnp.bfloat16).astype(jnp.float32)
    all_modes = jnp.arange(NX, dtype=jnp.int32)
    cas_x = cas_matrix(all_modes, NX)
    cells_y = velocity.shape[3]
    moved = []
    pressures = []
    for section in range(2):
        moving = velocity[section].astype(jnp.float32)
        along_x = jnp.einsum('ij,cjyz->ciyz', deriv_bf, moving, precision=highest)
        along_y = (jnp.roll(moving, -1, axis=2) - jnp.roll(moving, 1, axis=2)) * 0.5
        along_z = zdiff(moving)
        advection = moving[0] * along_x + moving[1] * along_y + moving[2] * along_z
        weights = fringe_weights(farm_split[0]) * float(section)
        outflow = velocity[0][:, NX - FR:].astype(jnp.float32)
        target = jnp.einsum('xj,cjyz->cxyz', weights, outflow, precision=highest)
        fringe = target - lax.optimization_barrier(jnp.sum(weights, axis=1))[None, :, None, None] * moving
        drag_field = turbine_field(turbine_cells, thrust, jnp.arange(cells_y, dtype=jnp.int32), NZ, cells_y) * float(section)
        thrust_force = -0.5 * drag_field * moving[0] * jnp.abs(moving[0])
        tendency = -advection + fringe
        tendency = jnp.concatenate([tendency[:1] + thrust_force[None], tendency[1:]], axis=0)
        ustar = (moving + time_step * tendency).astype(jnp.bfloat16)
        ustar_f = ustar.astype(jnp.float32)
        divergence = jnp.einsum('ij,jyz->iyz', deriv_bf, ustar_f[0], precision=highest)
        divergence = divergence + (jnp.roll(ustar_f[1], -1, axis=1) - jnp.roll(ustar_f[1], 1, axis=1)) * 0.5
        divergence = divergence + zdiff(ustar_f[2])
        source = divergence / time_step
        retained = kept_mask(all_modes, band_counts[section])
        spec = jnp.einsum('kx,xyz->kyz', cas_x, source, precision=highest) * retained[:, None, None]
        pres_modes, grad_modes = column_solve(spec, all_modes)
        pressure = jnp.einsum('kx,kyz->xyz', cas_x, pres_modes, precision=highest) / NX
        grad_y = jnp.einsum('kx,kyz->xyz', cas_x, grad_modes, precision=highest) / NX
        grad_x = jnp.einsum('ij,jyz->iyz', deriv_mat, pressure, precision=highest)
        grad_z = zdiff(pressure)
        newer = ustar_f - time_step * jnp.stack([grad_x, grad_y, grad_z], axis=0)
        moved.append(newer.astype(jnp.bfloat16))
        pressures.append(pressure)
    return (jnp.stack(moved, axis=0), jnp.stack(pressures, axis=0))
```

```python
import numpy as np
import jax
import jax.numpy as jnp
from jax import lax
from jax.sharding import PartitionSpec as P

NX = 1024
BAND = 32
NB = 10
FR = 32
DISK = 4
KX = 320
SLOTS = 2 * KX


highest = lax.Precision.HIGHEST
time_step = 0.25
screen = 0.01
fringe_rate = 2.0


def slot_modes():
    slots = np.arange(SLOTS)
    return np.where(slots < KX, slots, slots + NX - SLOTS)


def deriv_table():
    index = np.arange(NX)
    offset = (index[:, None] - index[None, :]) % NX
    angle = np.pi * offset / NX
    parity = 1.0 - 2.0 * (offset % 2)
    denom = np.where(offset == 0, 1.0, np.sin(angle))
    table = np.where(offset == 0, 0.0, 0.5 * parity * np.cos(angle) / denom)
    return jnp.asarray(table.astype(np.float32)).astype(jnp.bfloat16)


def cas_table(modes, length):
    cells = np.arange(length)
    angle = 2.0 * np.pi * ((modes[:, None] * cells[None, :]) % length) / length
    return np.cos(angle) + np.sin(angle)


def cosine_np(length):
    index = np.arange(length)
    angle = np.pi * index[:, None] * (2 * index[None, :] + 1) / (2 * length)
    scale = np.where(index == 0, np.sqrt(1.0 / length), np.sqrt(2.0 / length))
    return np.cos(angle) * scale[:, None]


def signed_np(length):
    index = np.arange(length)
    return np.where(index < length // 2, index, np.where(index > length // 2, index - length, 0))


def wave_square(mode_ids, length):
    folded = jnp.minimum(mode_ids, length - mode_ids).astype(jnp.float32)
    return (2.0 * jnp.pi * folded / length) ** 2


def kept_mask(mode_ids, counts):
    folded = jnp.minimum(mode_ids, NX - mode_ids)
    band_of = folded // BAND
    onehot = band_of[:, None] == jnp.arange(NB, dtype=jnp.int32)[None, :]
    limit_per = jnp.sum(jnp.where(onehot, counts[None, :], 0), axis=1)
    return ((folded < KX) & (folded % BAND < limit_per)).astype(jnp.float32)


def zdiff(field):
    zeros = jnp.zeros(field.shape[:-1] + (1,), jnp.float32)
    upper = jnp.concatenate([field[..., 1:], zeros], axis=-1)
    lower = jnp.concatenate([zeros, field[..., :-1]], axis=-1)
    return (upper - lower) * 0.5


def fringe_weights(split_at):
    cells = jnp.arange(NX, dtype=jnp.int32)[:, None]
    plane = jnp.arange(FR, dtype=jnp.int32)[None, :]
    rate = fringe_rate * jnp.sin(jnp.pi * (plane.astype(jnp.float32) + 0.5) / FR) ** 2
    inside = (cells == plane) | (cells == split_at + plane)
    return jnp.where(inside, rate, 0.0)


def turbine_field(cells, thrust, ycoord, count_z, span_total):
    onehot_x = (cells[:, 0][:, None] == jnp.arange(NX, dtype=jnp.int32)[None, :]).astype(
        jnp.float32
    ) * thrust[:, None]
    offset_y = (ycoord[None, :] - cells[:, 1][:, None]) % span_total
    onehot_y = ((offset_y <= DISK) | (offset_y >= span_total - DISK)).astype(jnp.float32)
    offset_z = jnp.abs(jnp.arange(count_z, dtype=jnp.int32)[None, :] - cells[:, 2][:, None])
    onehot_z = (offset_z <= DISK).astype(jnp.float32)
    cross_yz = (onehot_y[:, :, None] * onehot_z[:, None, :]).reshape(cells.shape[0], -1)
    field = jnp.dot(onehot_x.T, cross_yz, precision=highest)
    return field.reshape(NX, ycoord.shape[0], count_z)


def column_solve(columns, local_modes):
    cells_y = columns.shape[1]
    cells_z = columns.shape[2]
    ids_y = np.arange(cells_y)
    cas_y = jnp.asarray(cas_table(ids_y, cells_y).astype(np.float32))
    cos_z = jnp.asarray(cosine_np(cells_z).astype(np.float32))
    wave_y = 2.0 * np.pi * signed_np(cells_y) / cells_y
    back_p = cas_table(ids_y, cells_y) / cells_y
    back_g = wave_y[:, None] * cas_table((-ids_y) % cells_y, cells_y) / cells_y
    back_y = jnp.asarray(np.stack([back_p, back_g]).astype(np.float32))
    first = jnp.einsum("jy,ryz->rjz", cas_y, columns, precision=highest)
    second = jnp.einsum("rjz,mz->rjm", first, cos_z, precision=highest)
    kz_sq = (jnp.pi * jnp.arange(cells_z, dtype=jnp.int32).astype(jnp.float32) / cells_z) ** 2
    eigen = (
        wave_square(local_modes, NX)[:, None, None]
        + wave_square(jnp.arange(cells_y, dtype=jnp.int32), cells_y)[None, :, None]
        + kz_sq[None, None, :]
        + screen
    )
    p_hat = -second / eigen
    back = jnp.einsum("gjy,rjm->rgym", back_y, p_hat, precision=highest)
    return jnp.einsum("rgym,mz->rgyz", back, cos_z, precision=highest)


def local(velocity, thrust, band_counts, farm_split, turbine_cells):
    moving_bf = velocity[0]
    rows_here = moving_bf.shape[2]
    count_z = moving_bf.shape[3]
    col_index = lax.axis_index("col")
    cols = lax.axis_size("col")
    span_total = rows_here * cols
    farm_on = (lax.axis_index("sec") == 1).astype(jnp.float32)
    deriv_bf = deriv_table()
    modes_np = slot_modes()
    cas_x = jnp.asarray(cas_table(modes_np, NX).astype(np.float32))

    forward = [(i, (i + 1) % cols) for i in range(cols)]
    backward = [((i + 1) % cols, i) for i in range(cols)]
    low = lax.ppermute(moving_bf, "col", forward)
    high = lax.ppermute(moving_bf, "col", backward)
    outflow = lax.ppermute(moving_bf[:, NX - FR :], "sec", [(0, 1)])

    moving = moving_bf.astype(jnp.float32)
    along_x = jnp.einsum("ij,cjyz->ciyz", deriv_bf, moving_bf, preferred_element_type=jnp.float32)
    along_y = (high.astype(jnp.float32) - low.astype(jnp.float32)) * 0.5
    along_z = zdiff(moving)
    advection = moving[0] * along_x + moving[1] * along_y + moving[2] * along_z
    weights = fringe_weights(farm_split[0]) * farm_on
    target = jnp.einsum("xj,cjyz->cxyz", weights, outflow.astype(jnp.float32), precision=highest)
    fringe = target - jnp.sum(weights, axis=1)[None, :, None, None] * moving
    ycoord = col_index * rows_here + jnp.arange(rows_here, dtype=jnp.int32)
    drag_field = turbine_field(turbine_cells, thrust, ycoord, count_z, span_total) * farm_on
    thrust_force = -0.5 * drag_field * moving[0] * jnp.abs(moving[0])
    tendency = -advection + fringe
    tendency = jnp.concatenate([tendency[:1] + thrust_force[None], tendency[1:]], axis=0)
    ustar = (moving + time_step * tendency).astype(jnp.bfloat16)
    side_low = lax.ppermute(ustar[1], "col", forward).astype(jnp.float32)
    side_high = lax.ppermute(ustar[1], "col", backward).astype(jnp.float32)
    ustar_f = ustar.astype(jnp.float32)
    divergence = jnp.einsum("ij,jyz->iyz", deriv_bf, ustar[0], preferred_element_type=jnp.float32)
    divergence = divergence + (side_high - side_low) * 0.5
    divergence = divergence + zdiff(ustar_f[2])
    source = divergence / time_step
    modes = jnp.asarray(modes_np.astype(np.int32))
    retained = kept_mask(modes, band_counts[0])
    spec = jnp.einsum("kx,xyz->kyz", cas_x, source, precision=highest) * retained[:, None, None]
    columns = lax.all_to_all(spec, "col", split_axis=0, concat_axis=1, tiled=True)
    per_device = columns.shape[0]
    local_modes = lax.dynamic_slice_in_dim(modes, col_index * per_device, per_device)
    solved = column_solve(columns, local_modes)
    back = lax.all_to_all(solved, "col", split_axis=2, concat_axis=0, tiled=True)
    pres_modes = back[:, 0]
    grad_modes = back[:, 1]
    signed = np.where(modes_np < NX // 2, modes_np, modes_np - NX).astype(np.float32)
    mirrored = jnp.concatenate([pres_modes[:1], jnp.flip(pres_modes[1:], axis=0)], axis=0)
    dx_modes = -jnp.asarray(signed)[:, None, None] * mirrored
    stacked = jnp.stack([pres_modes, dx_modes, grad_modes], axis=0)
    fields = jnp.einsum("kx,gkyz->gxyz", cas_x, stacked, precision=highest) / NX
    pressure = fields[0]
    grad_x = fields[1]
    grad_y = fields[2]
    grad_z = zdiff(pressure)
    newer = ustar_f - time_step * jnp.stack([grad_x, grad_y, grad_z], axis=0)
    return (newer.astype(jnp.bfloat16)[None], pressure[None])


def solution(mesh):
    return jax.shard_map(
        local,
        mesh=mesh,
        in_specs=(P("sec", None, None, "col", None), P(), P("sec", None), P(), P()),
        out_specs=(P("sec", None, None, "col", None), P("sec", None, "col", None)),
        check_vma=False,
    )
```

```python
import numpy as np
import jax
import jax.numpy as jnp
from jax import lax
from jax.sharding import PartitionSpec as P

NX = 1024
BAND = 32
NB = 10
FR = 32
DISK = 4
KX = 320
SLOTS = 2 * KX


highest = lax.Precision.HIGHEST
time_step = 0.25
screen = 0.01
fringe_rate = 2.0


def slot_modes():
    slots = np.arange(SLOTS)
    return np.where(slots < KX, slots, slots + NX - SLOTS)


def deriv_table():
    index = np.arange(NX)
    offset = (index[:, None] - index[None, :]) % NX
    angle = np.pi * offset / NX
    parity = 1.0 - 2.0 * (offset % 2)
    denom = np.where(offset == 0, 1.0, np.sin(angle))
    table = np.where(offset == 0, 0.0, 0.5 * parity * np.cos(angle) / denom)
    return jnp.asarray(table.astype(np.float32)).astype(jnp.bfloat16)


def cas_table(modes, length):
    cells = np.arange(length)
    angle = 2.0 * np.pi * ((modes[:, None] * cells[None, :]) % length) / length
    return np.cos(angle) + np.sin(angle)


def cosine_np(length):
    index = np.arange(length)
    angle = np.pi * index[:, None] * (2 * index[None, :] + 1) / (2 * length)
    scale = np.where(index == 0, np.sqrt(1.0 / length), np.sqrt(2.0 / length))
    return np.cos(angle) * scale[:, None]


def signed_np(length):
    index = np.arange(length)
    return np.where(index < length // 2, index, np.where(index > length // 2, index - length, 0))


def wave_square(mode_ids, length):
    folded = jnp.minimum(mode_ids, length - mode_ids).astype(jnp.float32)
    return (2.0 * jnp.pi * folded / length) ** 2


def kept_mask(mode_ids, counts):
    folded = jnp.minimum(mode_ids, NX - mode_ids)
    band_of = folded // BAND
    onehot = band_of[:, None] == jnp.arange(NB, dtype=jnp.int32)[None, :]
    limit_per = jnp.sum(jnp.where(onehot, counts[None, :], 0), axis=1)
    return ((folded < KX) & (folded % BAND < limit_per)).astype(jnp.float32)


def zdiff(field):
    zeros = jnp.zeros(field.shape[:-1] + (1,), jnp.float32)
    upper = jnp.concatenate([field[..., 1:], zeros], axis=-1)
    lower = jnp.concatenate([zeros, field[..., :-1]], axis=-1)
    return (upper - lower) * 0.5


def fringe_weights(split_at):
    cells = jnp.arange(NX, dtype=jnp.int32)[:, None]
    plane = jnp.arange(FR, dtype=jnp.int32)[None, :]
    rate = fringe_rate * jnp.sin(jnp.pi * (plane.astype(jnp.float32) + 0.5) / FR) ** 2
    inside = (cells == plane) | (cells == split_at + plane)
    return jnp.where(inside, rate, 0.0)


def turbine_field(cells, thrust, ycoord, count_z, span_total):
    onehot_x = (cells[:, 0][:, None] == jnp.arange(NX, dtype=jnp.int32)[None, :]).astype(
        jnp.float32
    ) * thrust[:, None]
    offset_y = (ycoord[None, :] - cells[:, 1][:, None]) % span_total
    onehot_y = ((offset_y <= DISK) | (offset_y >= span_total - DISK)).astype(jnp.float32)
    offset_z = jnp.abs(jnp.arange(count_z, dtype=jnp.int32)[None, :] - cells[:, 2][:, None])
    onehot_z = (offset_z <= DISK).astype(jnp.float32)
    cross_yz = (onehot_y[:, :, None] * onehot_z[:, None, :]).reshape(cells.shape[0], -1)
    field = jnp.dot(onehot_x.T, cross_yz, precision=highest)
    return field.reshape(NX, ycoord.shape[0], count_z)


def column_solve(columns, local_modes):
    cells_y = columns.shape[1]
    cells_z = columns.shape[2]
    ids_y = np.arange(cells_y)
    cas_y = jnp.asarray(cas_table(ids_y, cells_y).astype(np.float32))
    cos_z = jnp.asarray(cosine_np(cells_z).astype(np.float32))
    wave_y = 2.0 * np.pi * signed_np(cells_y) / cells_y
    back_p = cas_table(ids_y, cells_y) / cells_y
    back_g = wave_y[:, None] * cas_table((-ids_y) % cells_y, cells_y) / cells_y
    back_y = jnp.asarray(np.stack([back_p, back_g]).astype(np.float32))
    first = jnp.einsum("jy,ryz->rjz", cas_y, columns, precision=highest)
    second = jnp.einsum("rjz,mz->rjm", first, cos_z, precision=highest)
    kz_sq = (jnp.pi * jnp.arange(cells_z, dtype=jnp.int32).astype(jnp.float32) / cells_z) ** 2
    eigen = (
        wave_square(local_modes, NX)[:, None, None]
        + wave_square(jnp.arange(cells_y, dtype=jnp.int32), cells_y)[None, :, None]
        + kz_sq[None, None, :]
        + screen
    )
    p_hat = -second / eigen
    back = jnp.einsum("gjy,rjm->rgym", back_y, p_hat, precision=highest)
    return jnp.einsum("rgym,mz->rgyz", back, cos_z, precision=highest)


def halo(block, cols):
    secs = lax.axis_size("sec")
    up = lambda s: [(s * cols + i, s * cols + (i + 1) % cols) for i in range(cols)]
    down = lambda s: [(s * cols + (i + 1) % cols, s * cols + i) for i in range(cols)]
    first = sum([up(s) if s % 2 == 0 else down(s) for s in range(secs)], [])
    second = sum([down(s) if s % 2 == 0 else up(s) for s in range(secs)], [])
    got_first = lax.ppermute(block, ("sec", "col"), first)
    got_second = lax.ppermute(block, ("sec", "col"), second)
    even = lax.axis_index("sec") % 2 == 0
    low = jnp.where(even, got_first, got_second)
    high = jnp.where(even, got_second, got_first)
    return low, high


def local(velocity, thrust, band_counts, farm_split, turbine_cells):
    moving_bf = velocity[0]
    rows_here = moving_bf.shape[2]
    count_z = moving_bf.shape[3]
    col_index = lax.axis_index("col")
    cols = lax.axis_size("col")
    span_total = rows_here * cols
    farm_on = (lax.axis_index("sec") == 1).astype(jnp.float32)
    deriv_bf = deriv_table()
    modes_np = slot_modes()
    cas_x = jnp.asarray(cas_table(modes_np, NX).astype(np.float32))

    low, high = halo(moving_bf, cols)
    outflow = lax.ppermute(moving_bf[:, NX - FR :], "sec", [(0, 1)])

    moving = moving_bf.astype(jnp.float32)
    along_x = jnp.einsum("ij,cjyz->ciyz", deriv_bf, moving_bf, preferred_element_type=jnp.float32)
    along_y = (high.astype(jnp.float32) - low.astype(jnp.float32)) * 0.5
    along_z = zdiff(moving)
    advection = moving[0] * along_x + moving[1] * along_y + moving[2] * along_z
    weights = fringe_weights(farm_split[0]) * farm_on
    target = jnp.einsum("xj,cjyz->cxyz", weights, outflow.astype(jnp.float32), precision=highest)
    fringe = target - jnp.sum(weights, axis=1)[None, :, None, None] * moving
    ycoord = col_index * rows_here + jnp.arange(rows_here, dtype=jnp.int32)
    drag_field = turbine_field(turbine_cells, thrust, ycoord, count_z, span_total) * farm_on
    thrust_force = -0.5 * drag_field * moving[0] * jnp.abs(moving[0])
    tendency = -advection + fringe
    tendency = jnp.concatenate([tendency[:1] + thrust_force[None], tendency[1:]], axis=0)
    ustar = (moving + time_step * tendency).astype(jnp.bfloat16)
    side_low, side_high = halo(ustar[1], cols)
    side_low = side_low.astype(jnp.float32)
    side_high = side_high.astype(jnp.float32)
    ustar_f = ustar.astype(jnp.float32)
    divergence = jnp.einsum("ij,jyz->iyz", deriv_bf, ustar[0], preferred_element_type=jnp.float32)
    divergence = divergence + (side_high - side_low) * 0.5
    divergence = divergence + zdiff(ustar_f[2])
    source = divergence / time_step
    modes = jnp.asarray(modes_np.astype(np.int32))
    retained = kept_mask(modes, band_counts[0])
    spec = jnp.einsum("kx,xyz->kyz", cas_x, source, precision=lax.Precision.HIGH) * retained[:, None, None]
    columns = lax.all_to_all(spec, "col", split_axis=0, concat_axis=1, tiled=True)
    per_device = columns.shape[0]
    local_modes = lax.dynamic_slice_in_dim(modes, col_index * per_device, per_device)
    solved = column_solve(columns, local_modes)
    back = lax.all_to_all(solved, "col", split_axis=2, concat_axis=0, tiled=True)
    pres_modes = back[:, 0]
    grad_modes = back[:, 1]
    signed = np.where(modes_np < NX // 2, modes_np, modes_np - NX).astype(np.float32)
    mirrored = jnp.concatenate([pres_modes[:1], jnp.flip(pres_modes[1:], axis=0)], axis=0)
    dx_modes = -jnp.asarray(signed)[:, None, None] * mirrored
    stacked = jnp.stack([pres_modes, dx_modes, grad_modes], axis=0)
    fields = jnp.einsum("kx,gkyz->gxyz", cas_x, stacked, precision=lax.Precision.HIGH) / NX
    pressure = fields[0]
    grad_x = fields[1]
    grad_y = fields[2]
    grad_z = zdiff(pressure)
    newer = ustar_f - time_step * jnp.stack([grad_x, grad_y, grad_z], axis=0)
    return (newer.astype(jnp.bfloat16)[None], pressure[None])


def solution(mesh):
    return jax.shard_map(
        local,
        mesh=mesh,
        in_specs=(P("sec", None, None, "col", None), P(), P("sec", None), P(), P()),
        out_specs=(P("sec", None, None, "col", None), P("sec", None, "col", None)),
        check_vma=False,
    )
```

```python
import numpy as np
import jax
import jax.numpy as jnp
from jax import lax
from jax.sharding import PartitionSpec as P

NX = 1024
BAND = 32
NB = 10
FR = 32
DISK = 4
KX = 320
SLOTS = 2 * KX


highest = lax.Precision.HIGHEST
time_step = 0.25
screen = 0.01
fringe_rate = 2.0


def slot_modes():
    slots = np.arange(SLOTS)
    return np.where(slots < KX, slots, slots + NX - SLOTS)


def deriv_table():
    index = np.arange(NX)
    offset = (index[:, None] - index[None, :]) % NX
    angle = np.pi * offset / NX
    parity = 1.0 - 2.0 * (offset % 2)
    denom = np.where(offset == 0, 1.0, np.sin(angle))
    table = np.where(offset == 0, 0.0, 0.5 * parity * np.cos(angle) / denom)
    return jnp.asarray(table.astype(np.float32)).astype(jnp.bfloat16)


def cas_table(modes, length):
    cells = np.arange(length)
    angle = 2.0 * np.pi * ((modes[:, None] * cells[None, :]) % length) / length
    return np.cos(angle) + np.sin(angle)


def cosine_np(length):
    index = np.arange(length)
    angle = np.pi * index[:, None] * (2 * index[None, :] + 1) / (2 * length)
    scale = np.where(index == 0, np.sqrt(1.0 / length), np.sqrt(2.0 / length))
    return np.cos(angle) * scale[:, None]


def signed_np(length):
    index = np.arange(length)
    return np.where(index < length // 2, index, np.where(index > length // 2, index - length, 0))


def wave_square(mode_ids, length):
    folded = jnp.minimum(mode_ids, length - mode_ids).astype(jnp.float32)
    return (2.0 * jnp.pi * folded / length) ** 2


def kept_mask(mode_ids, counts):
    folded = jnp.minimum(mode_ids, NX - mode_ids)
    band_of = folded // BAND
    onehot = band_of[:, None] == jnp.arange(NB, dtype=jnp.int32)[None, :]
    limit_per = jnp.sum(jnp.where(onehot, counts[None, :], 0), axis=1)
    return ((folded < KX) & (folded % BAND < limit_per)).astype(jnp.float32)


def zdiff(field):
    zeros = jnp.zeros(field.shape[:-1] + (1,), jnp.float32)
    upper = jnp.concatenate([field[..., 1:], zeros], axis=-1)
    lower = jnp.concatenate([zeros, field[..., :-1]], axis=-1)
    return (upper - lower) * 0.5


def fringe_weights(split_at):
    cells = jnp.arange(NX, dtype=jnp.int32)[:, None]
    plane = jnp.arange(FR, dtype=jnp.int32)[None, :]
    rate = fringe_rate * jnp.sin(jnp.pi * (plane.astype(jnp.float32) + 0.5) / FR) ** 2
    inside = (cells == plane) | (cells == split_at + plane)
    return jnp.where(inside, rate, 0.0)


def turbine_field(cells, thrust, ycoord, count_z, span_total):
    onehot_x = (cells[:, 0][:, None] == jnp.arange(NX, dtype=jnp.int32)[None, :]).astype(
        jnp.float32
    ) * thrust[:, None]
    offset_y = (ycoord[None, :] - cells[:, 1][:, None]) % span_total
    onehot_y = ((offset_y <= DISK) | (offset_y >= span_total - DISK)).astype(jnp.float32)
    offset_z = jnp.abs(jnp.arange(count_z, dtype=jnp.int32)[None, :] - cells[:, 2][:, None])
    onehot_z = (offset_z <= DISK).astype(jnp.float32)
    cross_yz = (onehot_y[:, :, None] * onehot_z[:, None, :]).reshape(cells.shape[0], -1)
    field = jnp.dot(onehot_x.T, cross_yz, precision=highest)
    return field.reshape(NX, ycoord.shape[0], count_z)


def column_solve(columns, local_modes):
    cells_y = columns.shape[1]
    cells_z = columns.shape[2]
    ids_y = np.arange(cells_y)
    cas_y = jnp.asarray(cas_table(ids_y, cells_y).astype(np.float32))
    cos_z = jnp.asarray(cosine_np(cells_z).astype(np.float32))
    wave_y = 2.0 * np.pi * signed_np(cells_y) / cells_y
    back_p = cas_table(ids_y, cells_y) / cells_y
    back_g = wave_y[:, None] * cas_table((-ids_y) % cells_y, cells_y) / cells_y
    back_y = jnp.asarray(np.stack([back_p, back_g]).astype(np.float32))
    first = jnp.einsum("jy,ryz->rjz", cas_y, columns, precision=highest)
    second = jnp.einsum("rjz,mz->rjm", first, cos_z, precision=highest)
    kz_sq = (jnp.pi * jnp.arange(cells_z, dtype=jnp.int32).astype(jnp.float32) / cells_z) ** 2
    eigen = (
        wave_square(local_modes, NX)[:, None, None]
        + wave_square(jnp.arange(cells_y, dtype=jnp.int32), cells_y)[None, :, None]
        + kz_sq[None, None, :]
        + screen
    )
    p_hat = -second / eigen
    back = jnp.einsum("gjy,rjm->rgym", back_y, p_hat, precision=highest)
    return jnp.einsum("rgym,mz->rgyz", back, cos_z, precision=highest)


COL = ("zh", "y", "x", "core")
INNER = ("x", "core")
OUTER = ("zh", "y")
ALL = ("sec",) + COL


def to_columns(spec):
    inner = lax.axis_size(INNER)
    outer = lax.axis_size(OUTER)
    depth = spec.shape[-1]
    parts = spec.reshape(outer, inner, -1, depth)
    parts = lax.all_to_all(parts, INNER, 1, 1, tiled=True)
    parts = lax.all_to_all(parts, OUTER, 0, 0, tiled=True)
    per = parts.shape[2]
    return parts.transpose(2, 0, 1, 3).reshape(per, outer * inner, depth)


def from_columns(solved):
    inner = lax.axis_size(INNER)
    outer = lax.axis_size(OUTER)
    per, fields, _, depth = solved.shape
    parts = solved.reshape(per, fields, outer, inner, depth)
    parts = lax.all_to_all(parts, OUTER, 2, 2, tiled=True)
    parts = lax.all_to_all(parts, INNER, 3, 3, tiled=True)
    return parts.transpose(2, 3, 0, 1, 4).reshape(outer * inner * per, fields, depth)


def halo(block, cols):
    secs = lax.axis_size("sec")
    up = lambda s: [(s * cols + i, s * cols + (i + 1) % cols) for i in range(cols)]
    down = lambda s: [(s * cols + (i + 1) % cols, s * cols + i) for i in range(cols)]
    first = sum([up(s) if s % 2 == 0 else down(s) for s in range(secs)], [])
    second = sum([down(s) if s % 2 == 0 else up(s) for s in range(secs)], [])
    got_first = lax.ppermute(block, ALL, first)
    got_second = lax.ppermute(block, ALL, second)
    even = lax.axis_index("sec") % 2 == 0
    low = jnp.where(even, got_first, got_second)
    high = jnp.where(even, got_second, got_first)
    return low, high


def local(velocity, thrust, band_counts, farm_split, turbine_cells):
    moving_bf = velocity[0]
    rows_here = moving_bf.shape[2]
    count_z = moving_bf.shape[3]
    col_index = lax.axis_index(COL)
    cols = lax.axis_size(COL)
    span_total = rows_here * cols
    farm_on = (lax.axis_index("sec") == 1).astype(jnp.float32)
    deriv_bf = deriv_table()
    modes_np = slot_modes()
    cas_x = jnp.asarray(cas_table(modes_np, NX).astype(np.float32))

    low, high = halo(moving_bf, cols)
    outflow = lax.ppermute(moving_bf[:, NX - FR :], "sec", [(0, 1)])

    moving = moving_bf.astype(jnp.float32)
    along_x = jnp.einsum("ij,cjyz->ciyz", deriv_bf, moving_bf, preferred_element_type=jnp.float32)
    along_y = (high.astype(jnp.float32) - low.astype(jnp.float32)) * 0.5
    along_z = zdiff(moving)
    advection = moving[0] * along_x + moving[1] * along_y + moving[2] * along_z
    weights = fringe_weights(farm_split[0]) * farm_on
    target = jnp.einsum("xj,cjyz->cxyz", weights, outflow.astype(jnp.float32), precision=highest)
    fringe = target - jnp.sum(weights, axis=1)[None, :, None, None] * moving
    ycoord = col_index * rows_here + jnp.arange(rows_here, dtype=jnp.int32)
    drag_field = turbine_field(turbine_cells, thrust, ycoord, count_z, span_total) * farm_on
    thrust_force = -0.5 * drag_field * moving[0] * jnp.abs(moving[0])
    tendency = -advection + fringe
    tendency = jnp.concatenate([tendency[:1] + thrust_force[None], tendency[1:]], axis=0)
    ustar = (moving + time_step * tendency).astype(jnp.bfloat16)
    side_low, side_high = halo(ustar[1], cols)
    side_low = side_low.astype(jnp.float32)
    side_high = side_high.astype(jnp.float32)
    ustar_f = ustar.astype(jnp.float32)
    divergence = jnp.einsum("ij,jyz->iyz", deriv_bf, ustar[0], preferred_element_type=jnp.float32)
    divergence = divergence + (side_high - side_low) * 0.5
    divergence = divergence + zdiff(ustar_f[2])
    source = divergence / time_step
    modes = jnp.asarray(modes_np.astype(np.int32))
    retained = kept_mask(modes, band_counts[0])
    spec = jnp.einsum("kx,xyz->kyz", cas_x, source, precision=lax.Precision.HIGH) * retained[:, None, None]
    columns = to_columns(spec[:, 0, :])
    per_device = columns.shape[0]
    local_modes = lax.dynamic_slice_in_dim(modes, col_index * per_device, per_device)
    solved = column_solve(columns, local_modes)
    back = from_columns(solved)
    pres_modes = back[:, 0][:, None]
    grad_modes = back[:, 1][:, None]
    signed = np.where(modes_np < NX // 2, modes_np, modes_np - NX).astype(np.float32)
    mirrored = jnp.concatenate([pres_modes[:1], jnp.flip(pres_modes[1:], axis=0)], axis=0)
    dx_modes = -jnp.asarray(signed)[:, None, None] * mirrored
    stacked = jnp.stack([pres_modes, dx_modes, grad_modes], axis=0)
    fields = jnp.einsum("kx,gkyz->gxyz", cas_x, stacked, precision=lax.Precision.HIGH) / NX
    pressure = fields[0]
    grad_x = fields[1]
    grad_y = fields[2]
    grad_z = zdiff(pressure)
    newer = ustar_f - time_step * jnp.stack([grad_x, grad_y, grad_z], axis=0)
    return (newer.astype(jnp.bfloat16)[None], pressure[None])


def solution(mesh):
    sizes = (mesh.shape["sec"], 4, 4, 4, 2)
    fine = jax.sharding.Mesh(mesh.devices.reshape(sizes), ALL)
    return jax.shard_map(
        local,
        mesh=fine,
        in_specs=(P("sec", None, None, COL, None), P(), P("sec", None), P(), P()),
        out_specs=(P("sec", None, None, COL, None), P("sec", None, COL, None)),
        check_vma=False,
    )
```

```python
import numpy as np
import jax
import jax.numpy as jnp
from jax import lax
from jax.sharding import PartitionSpec as P

NX = 1024
BAND = 32
NB = 10
FR = 32
DISK = 4
KX = 320
SLOTS = 2 * KX


highest = lax.Precision.HIGHEST
time_step = 0.25
screen = 0.01
fringe_rate = 2.0


def slot_modes():
    slots = np.arange(SLOTS)
    return np.where(slots < KX, slots, slots + NX - SLOTS)


def deriv_table():
    index = np.arange(NX)
    offset = (index[:, None] - index[None, :]) % NX
    angle = np.pi * offset / NX
    parity = 1.0 - 2.0 * (offset % 2)
    denom = np.where(offset == 0, 1.0, np.sin(angle))
    table = np.where(offset == 0, 0.0, 0.5 * parity * np.cos(angle) / denom)
    return jnp.asarray(table.astype(np.float32)).astype(jnp.bfloat16)


def cas_table(modes, length):
    cells = np.arange(length)
    angle = 2.0 * np.pi * ((modes[:, None] * cells[None, :]) % length) / length
    return np.cos(angle) + np.sin(angle)


def cosine_np(length):
    index = np.arange(length)
    angle = np.pi * index[:, None] * (2 * index[None, :] + 1) / (2 * length)
    scale = np.where(index == 0, np.sqrt(1.0 / length), np.sqrt(2.0 / length))
    return np.cos(angle) * scale[:, None]


def signed_np(length):
    index = np.arange(length)
    return np.where(index < length // 2, index, np.where(index > length // 2, index - length, 0))


def wave_square(mode_ids, length):
    folded = jnp.minimum(mode_ids, length - mode_ids).astype(jnp.float32)
    return (2.0 * jnp.pi * folded / length) ** 2


def kept_mask(mode_ids, counts):
    folded = jnp.minimum(mode_ids, NX - mode_ids)
    band_of = folded // BAND
    onehot = band_of[:, None] == jnp.arange(NB, dtype=jnp.int32)[None, :]
    limit_per = jnp.sum(jnp.where(onehot, counts[None, :], 0), axis=1)
    return ((folded < KX) & (folded % BAND < limit_per)).astype(jnp.float32)


def zdiff(field):
    zeros = jnp.zeros(field.shape[:-1] + (1,), jnp.float32)
    upper = jnp.concatenate([field[..., 1:], zeros], axis=-1)
    lower = jnp.concatenate([zeros, field[..., :-1]], axis=-1)
    return (upper - lower) * 0.5


def fringe_weights(split_at):
    cells = jnp.arange(NX, dtype=jnp.int32)[:, None]
    plane = jnp.arange(FR, dtype=jnp.int32)[None, :]
    rate = fringe_rate * jnp.sin(jnp.pi * (plane.astype(jnp.float32) + 0.5) / FR) ** 2
    inside = (cells == plane) | (cells == split_at + plane)
    return jnp.where(inside, rate, 0.0)


def turbine_field(cells, thrust, ycoord, count_z, span_total):
    onehot_x = (cells[:, 0][:, None] == jnp.arange(NX, dtype=jnp.int32)[None, :]).astype(
        jnp.float32
    ) * thrust[:, None]
    offset_y = (ycoord[None, :] - cells[:, 1][:, None]) % span_total
    onehot_y = ((offset_y <= DISK) | (offset_y >= span_total - DISK)).astype(jnp.float32)
    offset_z = jnp.abs(jnp.arange(count_z, dtype=jnp.int32)[None, :] - cells[:, 2][:, None])
    onehot_z = (offset_z <= DISK).astype(jnp.float32)
    cross_yz = (onehot_y[:, :, None] * onehot_z[:, None, :]).reshape(cells.shape[0], -1)
    field = jnp.dot(onehot_x.T, cross_yz, precision=highest)
    return field.reshape(NX, ycoord.shape[0], count_z)


def column_solve(columns, local_modes):
    cells_y = columns.shape[1]
    cells_z = columns.shape[2]
    ids_y = np.arange(cells_y)
    cas_y = jnp.asarray(cas_table(ids_y, cells_y).astype(np.float32))
    cos_z = jnp.asarray(cosine_np(cells_z).astype(np.float32))
    wave_y = 2.0 * np.pi * signed_np(cells_y) / cells_y
    back_p = cas_table(ids_y, cells_y) / cells_y
    back_g = wave_y[:, None] * cas_table((-ids_y) % cells_y, cells_y) / cells_y
    back_y = jnp.asarray(np.stack([back_p, back_g]).astype(np.float32))
    first = jnp.einsum("jy,ryz->rjz", cas_y, columns, precision=highest)
    second = jnp.einsum("rjz,mz->rjm", first, cos_z, precision=highest)
    kz_sq = (jnp.pi * jnp.arange(cells_z, dtype=jnp.int32).astype(jnp.float32) / cells_z) ** 2
    eigen = (
        wave_square(local_modes, NX)[:, None, None]
        + wave_square(jnp.arange(cells_y, dtype=jnp.int32), cells_y)[None, :, None]
        + kz_sq[None, None, :]
        + screen
    )
    p_hat = -second / eigen
    back = jnp.einsum("gjy,rjm->rgym", back_y, p_hat, precision=highest)
    return jnp.einsum("rgym,mz->rgyz", back, cos_z, precision=highest)


def halo(block, cols):
    secs = lax.axis_size("sec")
    up = lambda s: [(s * cols + i, s * cols + (i + 1) % cols) for i in range(cols)]
    down = lambda s: [(s * cols + (i + 1) % cols, s * cols + i) for i in range(cols)]
    first = sum([up(s) if s % 2 == 0 else down(s) for s in range(secs)], [])
    second = sum([down(s) if s % 2 == 0 else up(s) for s in range(secs)], [])
    got_first = lax.ppermute(block, ("sec", "col"), first)
    got_second = lax.ppermute(block, ("sec", "col"), second)
    even = lax.axis_index("sec") % 2 == 0
    low = jnp.where(even, got_first, got_second)
    high = jnp.where(even, got_second, got_first)
    return low, high


def local(velocity, thrust, band_counts, farm_split, turbine_cells):
    moving_bf = velocity[0]
    rows_here = moving_bf.shape[2]
    count_z = moving_bf.shape[3]
    col_index = lax.axis_index("col")
    cols = lax.axis_size("col")
    span_total = rows_here * cols
    farm_on = (lax.axis_index("sec") == 1).astype(jnp.float32)
    deriv_bf = deriv_table()
    modes_np = slot_modes()
    cas_x = jnp.asarray(cas_table(modes_np, NX).astype(np.float32))

    low, high = halo(moving_bf, cols)
    outflow = lax.ppermute(moving_bf[:, NX - FR :], "sec", [(0, 1)])

    moving = moving_bf.astype(jnp.float32)
    along_x = jnp.einsum("ij,cjyz->ciyz", deriv_bf, moving_bf, preferred_element_type=jnp.float32)
    along_y = (high.astype(jnp.float32) - low.astype(jnp.float32)) * 0.5
    along_z = zdiff(moving)
    advection = moving[0] * along_x + moving[1] * along_y + moving[2] * along_z
    weights = fringe_weights(farm_split[0]) * farm_on
    target = jnp.einsum("xj,cjyz->cxyz", weights, outflow.astype(jnp.float32), precision=highest)
    fringe = target - jnp.sum(weights, axis=1)[None, :, None, None] * moving
    ycoord = col_index * rows_here + jnp.arange(rows_here, dtype=jnp.int32)
    drag_field = turbine_field(turbine_cells, thrust, ycoord, count_z, span_total) * farm_on
    thrust_force = -0.5 * drag_field * moving[0] * jnp.abs(moving[0])
    tendency = -advection + fringe
    tendency = jnp.concatenate([tendency[:1] + thrust_force[None], tendency[1:]], axis=0)
    ustar = (moving + time_step * tendency).astype(jnp.bfloat16)
    side_low, side_high = halo(ustar[1], cols)
    side_low = side_low.astype(jnp.float32)
    side_high = side_high.astype(jnp.float32)
    ustar_f = ustar.astype(jnp.float32)
    divergence = jnp.einsum("ij,jyz->iyz", deriv_bf, ustar[0], preferred_element_type=jnp.float32)
    divergence = divergence + (side_high - side_low) * 0.5
    divergence = divergence + zdiff(ustar_f[2])
    source = divergence / time_step
    modes = jnp.asarray(modes_np.astype(np.int32))
    retained = kept_mask(modes, band_counts[0])
    spec = jnp.einsum("kx,xyz->kyz", cas_x, source, precision=lax.Precision.HIGH) * retained[:, None, None]
    columns = lax.all_to_all(spec, "col", split_axis=0, concat_axis=1, tiled=True)
    per_device = columns.shape[0]
    local_modes = lax.dynamic_slice_in_dim(modes, col_index * per_device, per_device)
    solved = column_solve(columns, local_modes)
    pres_modes = lax.all_to_all(solved[:, 0], "col", split_axis=1, concat_axis=0, tiled=True)
    grad_modes = lax.all_to_all(solved[:, 1], "col", split_axis=1, concat_axis=0, tiled=True)
    signed = np.where(modes_np < NX // 2, modes_np, modes_np - NX).astype(np.float32)
    mirrored = jnp.concatenate([pres_modes[:1], jnp.flip(pres_modes[1:], axis=0)], axis=0)
    dx_modes = -jnp.asarray(signed)[:, None, None] * mirrored
    stacked = jnp.stack([pres_modes, dx_modes], axis=0)
    fields = jnp.einsum("kx,gkyz->gxyz", cas_x, stacked, precision=lax.Precision.HIGH) / NX
    pressure = fields[0]
    grad_x = fields[1]
    grad_y = jnp.einsum("kx,kyz->xyz", cas_x, grad_modes, precision=lax.Precision.HIGH) / NX
    grad_z = zdiff(pressure)
    newer = ustar_f - time_step * jnp.stack([grad_x, grad_y, grad_z], axis=0)
    return (newer.astype(jnp.bfloat16)[None], pressure[None])


def solution(mesh):
    return jax.shard_map(
        local,
        mesh=mesh,
        in_specs=(P("sec", None, None, "col", None), P(), P("sec", None), P(), P()),
        out_specs=(P("sec", None, None, "col", None), P("sec", None, "col", None)),
        check_vma=False,
    )
```

```python
import numpy as np
import jax
import jax.numpy as jnp
from jax import lax
from jax.sharding import PartitionSpec as P

NX = 1024
BAND = 32
NB = 10
FR = 32
DISK = 4
KX = 320
SLOTS = 2 * KX


highest = lax.Precision.HIGHEST
time_step = 0.25
screen = 0.01
fringe_rate = 2.0


def slot_modes():
    slots = np.arange(SLOTS)
    return np.where(slots < KX, slots, slots + NX - SLOTS)


def deriv_table():
    index = np.arange(NX)
    offset = (index[:, None] - index[None, :]) % NX
    angle = np.pi * offset / NX
    parity = 1.0 - 2.0 * (offset % 2)
    denom = np.where(offset == 0, 1.0, np.sin(angle))
    table = np.where(offset == 0, 0.0, 0.5 * parity * np.cos(angle) / denom)
    return jnp.asarray(table.astype(np.float32)).astype(jnp.bfloat16)


def cas_table(modes, length):
    cells = np.arange(length)
    angle = 2.0 * np.pi * ((modes[:, None] * cells[None, :]) % length) / length
    return np.cos(angle) + np.sin(angle)


def cosine_np(length):
    index = np.arange(length)
    angle = np.pi * index[:, None] * (2 * index[None, :] + 1) / (2 * length)
    scale = np.where(index == 0, np.sqrt(1.0 / length), np.sqrt(2.0 / length))
    return np.cos(angle) * scale[:, None]


def signed_np(length):
    index = np.arange(length)
    return np.where(index < length // 2, index, np.where(index > length // 2, index - length, 0))


def wave_square(mode_ids, length):
    folded = jnp.minimum(mode_ids, length - mode_ids).astype(jnp.float32)
    return (2.0 * jnp.pi * folded / length) ** 2


def kept_mask(mode_ids, counts):
    folded = jnp.minimum(mode_ids, NX - mode_ids)
    band_of = folded // BAND
    onehot = band_of[:, None] == jnp.arange(NB, dtype=jnp.int32)[None, :]
    limit_per = jnp.sum(jnp.where(onehot, counts[None, :], 0), axis=1)
    return ((folded < KX) & (folded % BAND < limit_per)).astype(jnp.float32)


def zdiff(field):
    zeros = jnp.zeros(field.shape[:-1] + (1,), jnp.float32)
    upper = jnp.concatenate([field[..., 1:], zeros], axis=-1)
    lower = jnp.concatenate([zeros, field[..., :-1]], axis=-1)
    return (upper - lower) * 0.5


def fringe_weights(split_at):
    cells = jnp.arange(NX, dtype=jnp.int32)[:, None]
    plane = jnp.arange(FR, dtype=jnp.int32)[None, :]
    rate = fringe_rate * jnp.sin(jnp.pi * (plane.astype(jnp.float32) + 0.5) / FR) ** 2
    inside = (cells == plane) | (cells == split_at + plane)
    return jnp.where(inside, rate, 0.0)


def turbine_field(cells, thrust, ycoord, count_z, span_total):
    onehot_x = (cells[:, 0][:, None] == jnp.arange(NX, dtype=jnp.int32)[None, :]).astype(
        jnp.float32
    ) * thrust[:, None]
    offset_y = (ycoord[None, :] - cells[:, 1][:, None]) % span_total
    onehot_y = ((offset_y <= DISK) | (offset_y >= span_total - DISK)).astype(jnp.float32)
    offset_z = jnp.abs(jnp.arange(count_z, dtype=jnp.int32)[None, :] - cells[:, 2][:, None])
    onehot_z = (offset_z <= DISK).astype(jnp.float32)
    cross_yz = (onehot_y[:, :, None] * onehot_z[:, None, :]).reshape(cells.shape[0], -1)
    field = jnp.dot(onehot_x.T, cross_yz, precision=highest)
    return field.reshape(NX, ycoord.shape[0], count_z)


def column_solve(columns, local_modes):
    cells_y = columns.shape[1]
    cells_z = columns.shape[2]
    ids_y = np.arange(cells_y)
    cas_y = jnp.asarray(cas_table(ids_y, cells_y).astype(np.float32))
    cos_z = jnp.asarray(cosine_np(cells_z).astype(np.float32))
    wave_y = 2.0 * np.pi * signed_np(cells_y) / cells_y
    back_p = cas_table(ids_y, cells_y) / cells_y
    back_g = wave_y[:, None] * cas_table((-ids_y) % cells_y, cells_y) / cells_y
    back_y = jnp.asarray(np.stack([back_p, back_g]).astype(np.float32))
    first = jnp.einsum("jy,ryz->rjz", cas_y, columns, precision=highest)
    second = jnp.einsum("rjz,mz->rjm", first, cos_z, precision=highest)
    kz_sq = (jnp.pi * jnp.arange(cells_z, dtype=jnp.int32).astype(jnp.float32) / cells_z) ** 2
    eigen = (
        wave_square(local_modes, NX)[:, None, None]
        + wave_square(jnp.arange(cells_y, dtype=jnp.int32), cells_y)[None, :, None]
        + kz_sq[None, None, :]
        + screen
    )
    p_hat = -second / eigen
    back = jnp.einsum("gjy,rjm->rgym", back_y, p_hat, precision=highest)
    return jnp.einsum("rgym,mz->rgyz", back, cos_z, precision=highest)


def halo(block, cols):
    secs = lax.axis_size("sec")
    up = lambda s: [(s * cols + i, s * cols + (i + 1) % cols) for i in range(cols)]
    down = lambda s: [(s * cols + (i + 1) % cols, s * cols + i) for i in range(cols)]
    first = sum([up(s) if s % 2 == 0 else down(s) for s in range(secs)], [])
    second = sum([down(s) if s % 2 == 0 else up(s) for s in range(secs)], [])
    got_first = lax.ppermute(block, ("sec", "col"), first)
    got_second = lax.ppermute(block, ("sec", "col"), second)
    even = lax.axis_index("sec") % 2 == 0
    low = jnp.where(even, got_first, got_second)
    high = jnp.where(even, got_second, got_first)
    return low, high


def local(velocity, thrust, band_counts, farm_split, turbine_cells):
    moving_bf = velocity[0]
    rows_here = moving_bf.shape[2]
    count_z = moving_bf.shape[3]
    col_index = lax.axis_index("col")
    cols = lax.axis_size("col")
    span_total = rows_here * cols
    farm_on = (lax.axis_index("sec") == 1).astype(jnp.float32)
    deriv_bf = deriv_table()
    modes_np = slot_modes()
    cas_x = jnp.asarray(cas_table(modes_np, NX).astype(np.float32))

    low, high = halo(moving_bf, cols)
    outflow = lax.ppermute(moving_bf[:, NX - FR :], "sec", [(0, 1)])

    moving = moving_bf.astype(jnp.float32)
    along_x = jnp.einsum("ij,cjyz->ciyz", deriv_bf, moving_bf, preferred_element_type=jnp.float32)
    along_y = (high.astype(jnp.float32) - low.astype(jnp.float32)) * 0.5
    along_z = zdiff(moving)
    advection = moving[0] * along_x + moving[1] * along_y + moving[2] * along_z
    weights = fringe_weights(farm_split[0]) * farm_on
    target = jnp.einsum("xj,cjyz->cxyz", weights, outflow.astype(jnp.float32), precision=highest)
    fringe = target - jnp.sum(weights, axis=1)[None, :, None, None] * moving
    ycoord = col_index * rows_here + jnp.arange(rows_here, dtype=jnp.int32)
    drag_field = turbine_field(turbine_cells, thrust, ycoord, count_z, span_total) * farm_on
    thrust_force = -0.5 * drag_field * moving[0] * jnp.abs(moving[0])
    tendency = -advection + fringe
    tendency = jnp.concatenate([tendency[:1] + thrust_force[None], tendency[1:]], axis=0)
    ustar = (moving + time_step * tendency).astype(jnp.bfloat16)
    ustar_f = ustar.astype(jnp.float32)
    divergence = jnp.einsum("ij,jyz->iyz", deriv_bf, ustar[0], preferred_element_type=jnp.float32)
    divergence = divergence + zdiff(ustar_f[2])
    parts = jnp.stack([divergence, ustar_f[1]], axis=0) / time_step
    spec = jnp.einsum("kx,gxyz->gkyz", cas_x, parts, precision=lax.Precision.HIGH)
    both = lax.all_to_all(spec, "col", split_axis=1, concat_axis=2, tiled=True)
    per_device = both.shape[1]
    modes = jnp.asarray(modes_np.astype(np.int32))
    local_modes = lax.dynamic_slice_in_dim(modes, col_index * per_device, per_device)
    retained = kept_mask(local_modes, band_counts[0])
    spanwise = both[1]
    spanwise_diff = (jnp.roll(spanwise, -1, axis=1) - jnp.roll(spanwise, 1, axis=1)) * 0.5
    columns = (both[0] + spanwise_diff) * retained[:, None, None]
    solved = column_solve(columns, local_modes)
    back = lax.all_to_all(solved, "col", split_axis=2, concat_axis=0, tiled=True)
    pres_modes = back[:, 0]
    grad_modes = back[:, 1]
    signed = np.where(modes_np < NX // 2, modes_np, modes_np - NX).astype(np.float32)
    mirrored = jnp.concatenate([pres_modes[:1], jnp.flip(pres_modes[1:], axis=0)], axis=0)
    dx_modes = -jnp.asarray(signed)[:, None, None] * mirrored
    stacked = jnp.stack([pres_modes, dx_modes, grad_modes], axis=0)
    fields = jnp.einsum("kx,gkyz->gxyz", cas_x, stacked, precision=lax.Precision.HIGH) / NX
    pressure = fields[0]
    grad_x = fields[1]
    grad_y = fields[2]
    grad_z = zdiff(pressure)
    newer = ustar_f - time_step * jnp.stack([grad_x, grad_y, grad_z], axis=0)
    return (newer.astype(jnp.bfloat16)[None], pressure[None])


def solution(mesh):
    return jax.shard_map(
        local,
        mesh=mesh,
        in_specs=(P("sec", None, None, "col", None), P(), P("sec", None), P(), P()),
        out_specs=(P("sec", None, None, "col", None), P("sec", None, "col", None)),
        check_vma=False,
    )
```

```python
import numpy as np
import jax
import jax.numpy as jnp
from jax import lax
from jax.sharding import PartitionSpec as P

NX = 1024
BAND = 32
NB = 10
FR = 32
DISK = 4
KX = 320
SLOTS = 2 * KX


highest = lax.Precision.HIGHEST
time_step = 0.25
screen = 0.01
fringe_rate = 2.0


def slot_modes():
    slots = np.arange(SLOTS)
    return np.where(slots < KX, slots, slots + NX - SLOTS)


def deriv_table():
    index = np.arange(NX)
    offset = (index[:, None] - index[None, :]) % NX
    angle = np.pi * offset / NX
    parity = 1.0 - 2.0 * (offset % 2)
    denom = np.where(offset == 0, 1.0, np.sin(angle))
    table = np.where(offset == 0, 0.0, 0.5 * parity * np.cos(angle) / denom)
    return jnp.asarray(table.astype(np.float32)).astype(jnp.bfloat16)


def cas_table(modes, length):
    cells = np.arange(length)
    angle = 2.0 * np.pi * ((modes[:, None] * cells[None, :]) % length) / length
    return np.cos(angle) + np.sin(angle)


def cosine_np(length):
    index = np.arange(length)
    angle = np.pi * index[:, None] * (2 * index[None, :] + 1) / (2 * length)
    scale = np.where(index == 0, np.sqrt(1.0 / length), np.sqrt(2.0 / length))
    return np.cos(angle) * scale[:, None]


def signed_np(length):
    index = np.arange(length)
    return np.where(index < length // 2, index, np.where(index > length // 2, index - length, 0))


def wave_square(mode_ids, length):
    folded = jnp.minimum(mode_ids, length - mode_ids).astype(jnp.float32)
    return (2.0 * jnp.pi * folded / length) ** 2


def kept_mask(mode_ids, counts):
    folded = jnp.minimum(mode_ids, NX - mode_ids)
    band_of = folded // BAND
    onehot = band_of[:, None] == jnp.arange(NB, dtype=jnp.int32)[None, :]
    limit_per = jnp.sum(jnp.where(onehot, counts[None, :], 0), axis=1)
    return ((folded < KX) & (folded % BAND < limit_per)).astype(jnp.float32)


def zdiff(field):
    zeros = jnp.zeros(field.shape[:-1] + (1,), jnp.float32)
    upper = jnp.concatenate([field[..., 1:], zeros], axis=-1)
    lower = jnp.concatenate([zeros, field[..., :-1]], axis=-1)
    return (upper - lower) * 0.5


def fringe_weights(split_at):
    cells = jnp.arange(NX, dtype=jnp.int32)[:, None]
    plane = jnp.arange(FR, dtype=jnp.int32)[None, :]
    rate = fringe_rate * jnp.sin(jnp.pi * (plane.astype(jnp.float32) + 0.5) / FR) ** 2
    inside = (cells == plane) | (cells == split_at + plane)
    return jnp.where(inside, rate, 0.0)


def turbine_field(cells, thrust, ycoord, count_z, span_total):
    onehot_x = (cells[:, 0][:, None] == jnp.arange(NX, dtype=jnp.int32)[None, :]).astype(
        jnp.float32
    ) * thrust[:, None]
    offset_y = (ycoord[None, :] - cells[:, 1][:, None]) % span_total
    onehot_y = ((offset_y <= DISK) | (offset_y >= span_total - DISK)).astype(jnp.float32)
    offset_z = jnp.abs(jnp.arange(count_z, dtype=jnp.int32)[None, :] - cells[:, 2][:, None])
    onehot_z = (offset_z <= DISK).astype(jnp.float32)
    cross_yz = (onehot_y[:, :, None] * onehot_z[:, None, :]).reshape(cells.shape[0], -1)
    field = jnp.dot(onehot_x.T, cross_yz, precision=highest)
    return field.reshape(NX, ycoord.shape[0], count_z)


def column_solve(columns, local_modes):
    cells_y = columns.shape[1]
    cells_z = columns.shape[2]
    ids_y = np.arange(cells_y)
    cas_y = jnp.asarray(cas_table(ids_y, cells_y).astype(np.float32))
    cos_z = jnp.asarray(cosine_np(cells_z).astype(np.float32))
    wave_y = 2.0 * np.pi * signed_np(cells_y) / cells_y
    back_p = cas_table(ids_y, cells_y) / cells_y
    back_g = wave_y[:, None] * cas_table((-ids_y) % cells_y, cells_y) / cells_y
    back_y = jnp.asarray(np.stack([back_p, back_g]).astype(np.float32))
    first = jnp.einsum("jy,ryz->rjz", cas_y, columns, precision=highest)
    second = jnp.einsum("rjz,mz->rjm", first, cos_z, precision=highest)
    kz_sq = (jnp.pi * jnp.arange(cells_z, dtype=jnp.int32).astype(jnp.float32) / cells_z) ** 2
    eigen = (
        wave_square(local_modes, NX)[:, None, None]
        + wave_square(jnp.arange(cells_y, dtype=jnp.int32), cells_y)[None, :, None]
        + kz_sq[None, None, :]
        + screen
    )
    p_hat = -second / eigen
    back = jnp.einsum("gjy,rjm->rgym", back_y, p_hat, precision=highest)
    return jnp.einsum("rgym,mz->rgyz", back, cos_z, precision=highest)


DIGITS = (4, 4, 4, 2)


def exchange(block, cols):
    col = lax.axis_index("col")
    for dim, n in enumerate(DIGITS):
        stride = int(np.prod(DIGITS[dim + 1 :]))
        mine = (col // stride) % n
        out = block
        for k in range(1, n):
            sent = lax.dynamic_index_in_dim(block, (mine + k) % n, dim, keepdims=True)
            pairs = [(c, c + (((c // stride) % n + k) % n - (c // stride) % n) * stride) for c in range(cols)]
            got = lax.ppermute(sent, "col", pairs)
            out = lax.dynamic_update_index_in_dim(out, got, (mine - k) % n, dim)
        block = out
    return block


def to_columns(spec):
    slots, depth = spec.shape
    cols = int(np.prod(DIGITS))
    per = slots // cols
    t = exchange(spec.reshape(DIGITS + (per, depth)), cols)
    return t.reshape(cols, per, depth).transpose(1, 0, 2)


def from_columns(solved):
    per, fields, cols, depth = solved.shape
    t = solved.reshape((per, fields) + DIGITS + (depth,))
    t = t.transpose(2, 3, 4, 5, 0, 1, 6)
    t = exchange(t, cols)
    return t.reshape(cols * per, fields, depth)


def halo(block, cols):
    secs = lax.axis_size("sec")
    up = lambda s: [(s * cols + i, s * cols + (i + 1) % cols) for i in range(cols)]
    down = lambda s: [(s * cols + (i + 1) % cols, s * cols + i) for i in range(cols)]
    first = sum([up(s) if s % 2 == 0 else down(s) for s in range(secs)], [])
    second = sum([down(s) if s % 2 == 0 else up(s) for s in range(secs)], [])
    got_first = lax.ppermute(block, ("sec", "col"), first)
    got_second = lax.ppermute(block, ("sec", "col"), second)
    even = lax.axis_index("sec") % 2 == 0
    low = jnp.where(even, got_first, got_second)
    high = jnp.where(even, got_second, got_first)
    return low, high


def local(velocity, thrust, band_counts, farm_split, turbine_cells):
    moving_bf = velocity[0]
    rows_here = moving_bf.shape[2]
    count_z = moving_bf.shape[3]
    col_index = lax.axis_index("col")
    cols = lax.axis_size("col")
    span_total = rows_here * cols
    farm_on = (lax.axis_index("sec") == 1).astype(jnp.float32)
    deriv_bf = deriv_table()
    modes_np = slot_modes()
    cas_x = jnp.asarray(cas_table(modes_np, NX).astype(np.float32))

    low, high = halo(moving_bf, cols)
    outflow = lax.ppermute(moving_bf[:, NX - FR :], "sec", [(0, 1)])

    moving = moving_bf.astype(jnp.float32)
    along_x = jnp.einsum("ij,cjyz->ciyz", deriv_bf, moving_bf, preferred_element_type=jnp.float32)
    along_y = (high.astype(jnp.float32) - low.astype(jnp.float32)) * 0.5
    along_z = zdiff(moving)
    advection = moving[0] * along_x + moving[1] * along_y + moving[2] * along_z
    weights = fringe_weights(farm_split[0]) * farm_on
    target = jnp.einsum("xj,cjyz->cxyz", weights, outflow.astype(jnp.float32), precision=highest)
    fringe = target - jnp.sum(weights, axis=1)[None, :, None, None] * moving
    ycoord = col_index * rows_here + jnp.arange(rows_here, dtype=jnp.int32)
    drag_field = turbine_field(turbine_cells, thrust, ycoord, count_z, span_total) * farm_on
    thrust_force = -0.5 * drag_field * moving[0] * jnp.abs(moving[0])
    tendency = -advection + fringe
    tendency = jnp.concatenate([tendency[:1] + thrust_force[None], tendency[1:]], axis=0)
    ustar = (moving + time_step * tendency).astype(jnp.bfloat16)
    side_low, side_high = halo(ustar[1], cols)
    side_low = side_low.astype(jnp.float32)
    side_high = side_high.astype(jnp.float32)
    ustar_f = ustar.astype(jnp.float32)
    divergence = jnp.einsum("ij,jyz->iyz", deriv_bf, ustar[0], preferred_element_type=jnp.float32)
    divergence = divergence + (side_high - side_low) * 0.5
    divergence = divergence + zdiff(ustar_f[2])
    source = divergence / time_step
    modes = jnp.asarray(modes_np.astype(np.int32))
    retained = kept_mask(modes, band_counts[0])
    spec = jnp.einsum("kx,xyz->kyz", cas_x, source, precision=lax.Precision.HIGH) * retained[:, None, None]
    columns = to_columns(spec[:, 0, :])
    per_device = columns.shape[0]
    local_modes = lax.dynamic_slice_in_dim(modes, col_index * per_device, per_device)
    solved = column_solve(columns, local_modes)
    back = from_columns(solved)
    pres_modes = back[:, 0][:, None]
    grad_modes = back[:, 1][:, None]
    signed = np.where(modes_np < NX // 2, modes_np, modes_np - NX).astype(np.float32)
    mirrored = jnp.concatenate([pres_modes[:1], jnp.flip(pres_modes[1:], axis=0)], axis=0)
    dx_modes = -jnp.asarray(signed)[:, None, None] * mirrored
    stacked = jnp.stack([pres_modes, dx_modes, grad_modes], axis=0)
    fields = jnp.einsum("kx,gkyz->gxyz", cas_x, stacked, precision=lax.Precision.HIGH) / NX
    pressure = fields[0]
    grad_x = fields[1]
    grad_y = fields[2]
    grad_z = zdiff(pressure)
    newer = ustar_f - time_step * jnp.stack([grad_x, grad_y, grad_z], axis=0)
    return (newer.astype(jnp.bfloat16)[None], pressure[None])


def solution(mesh):
    return jax.shard_map(
        local,
        mesh=mesh,
        in_specs=(P("sec", None, None, "col", None), P(), P("sec", None), P(), P()),
        out_specs=(P("sec", None, None, "col", None), P("sec", None, "col", None)),
        check_vma=False,
    )
```

```python
import numpy as np
import jax
import jax.numpy as jnp
from jax import lax
from jax.sharding import PartitionSpec as P

NX = 1024
BAND = 32
NB = 10
FR = 32
DISK = 4
KX = 320
SLOTS = 2 * KX


highest = lax.Precision.HIGHEST
time_step = 0.25
screen = 0.01
fringe_rate = 2.0


def slot_modes():
    slots = np.arange(SLOTS)
    return np.where(slots < KX, slots, slots + NX - SLOTS)


def deriv_table():
    index = np.arange(NX)
    offset = (index[:, None] - index[None, :]) % NX
    angle = np.pi * offset / NX
    parity = 1.0 - 2.0 * (offset % 2)
    denom = np.where(offset == 0, 1.0, np.sin(angle))
    table = np.where(offset == 0, 0.0, 0.5 * parity * np.cos(angle) / denom)
    return jnp.asarray(table.astype(np.float32)).astype(jnp.bfloat16)


def cas_table(modes, length):
    cells = np.arange(length)
    angle = 2.0 * np.pi * ((modes[:, None] * cells[None, :]) % length) / length
    return np.cos(angle) + np.sin(angle)


def cosine_np(length):
    index = np.arange(length)
    angle = np.pi * index[:, None] * (2 * index[None, :] + 1) / (2 * length)
    scale = np.where(index == 0, np.sqrt(1.0 / length), np.sqrt(2.0 / length))
    return np.cos(angle) * scale[:, None]


def signed_np(length):
    index = np.arange(length)
    return np.where(index < length // 2, index, np.where(index > length // 2, index - length, 0))


def wave_square(mode_ids, length):
    folded = jnp.minimum(mode_ids, length - mode_ids).astype(jnp.float32)
    return (2.0 * jnp.pi * folded / length) ** 2


def kept_mask(mode_ids, counts):
    folded = jnp.minimum(mode_ids, NX - mode_ids)
    band_of = folded // BAND
    onehot = band_of[:, None] == jnp.arange(NB, dtype=jnp.int32)[None, :]
    limit_per = jnp.sum(jnp.where(onehot, counts[None, :], 0), axis=1)
    return ((folded < KX) & (folded % BAND < limit_per)).astype(jnp.float32)


def zdiff(field):
    zeros = jnp.zeros(field.shape[:-1] + (1,), jnp.float32)
    upper = jnp.concatenate([field[..., 1:], zeros], axis=-1)
    lower = jnp.concatenate([zeros, field[..., :-1]], axis=-1)
    return (upper - lower) * 0.5


def fringe_weights(split_at):
    cells = jnp.arange(NX, dtype=jnp.int32)[:, None]
    plane = jnp.arange(FR, dtype=jnp.int32)[None, :]
    rate = fringe_rate * jnp.sin(jnp.pi * (plane.astype(jnp.float32) + 0.5) / FR) ** 2
    inside = (cells == plane) | (cells == split_at + plane)
    return jnp.where(inside, rate, 0.0)


def turbine_field(cells, thrust, ycoord, count_z, span_total):
    onehot_x = (cells[:, 0][:, None] == jnp.arange(NX, dtype=jnp.int32)[None, :]).astype(
        jnp.float32
    ) * thrust[:, None]
    offset_y = (ycoord[None, :] - cells[:, 1][:, None]) % span_total
    onehot_y = ((offset_y <= DISK) | (offset_y >= span_total - DISK)).astype(jnp.float32)
    offset_z = jnp.abs(jnp.arange(count_z, dtype=jnp.int32)[None, :] - cells[:, 2][:, None])
    onehot_z = (offset_z <= DISK).astype(jnp.float32)
    cross_yz = (onehot_y[:, :, None] * onehot_z[:, None, :]).reshape(cells.shape[0], -1)
    field = jnp.dot(onehot_x.T, cross_yz, precision=highest)
    return field.reshape(NX, ycoord.shape[0], count_z)


def column_solve(columns, local_modes):
    cells_y = columns.shape[1]
    cells_z = columns.shape[2]
    ids_y = np.arange(cells_y)
    cas_y = jnp.asarray(cas_table(ids_y, cells_y).astype(np.float32))
    cos_z = jnp.asarray(cosine_np(cells_z).astype(np.float32))
    wave_y = 2.0 * np.pi * signed_np(cells_y) / cells_y
    back_p = cas_table(ids_y, cells_y) / cells_y
    back_g = wave_y[:, None] * cas_table((-ids_y) % cells_y, cells_y) / cells_y
    back_y = jnp.asarray(np.stack([back_p, back_g]).astype(np.float32))
    first = jnp.einsum("jy,ryz->rjz", cas_y, columns, precision=lax.Precision.HIGH)
    second = jnp.einsum("rjz,mz->rjm", first, cos_z, precision=lax.Precision.HIGH)
    kz_sq = (jnp.pi * jnp.arange(cells_z, dtype=jnp.int32).astype(jnp.float32) / cells_z) ** 2
    eigen = (
        wave_square(local_modes, NX)[:, None, None]
        + wave_square(jnp.arange(cells_y, dtype=jnp.int32), cells_y)[None, :, None]
        + kz_sq[None, None, :]
        + screen
    )
    p_hat = -second / eigen
    back = jnp.einsum("gjy,rjm->rgym", back_y, p_hat, precision=lax.Precision.HIGH)
    return jnp.einsum("rgym,mz->rgyz", back, cos_z, precision=lax.Precision.HIGH)


def halo(block, cols):
    secs = lax.axis_size("sec")
    up = lambda s: [(s * cols + i, s * cols + (i + 1) % cols) for i in range(cols)]
    down = lambda s: [(s * cols + (i + 1) % cols, s * cols + i) for i in range(cols)]
    first = sum([up(s) if s % 2 == 0 else down(s) for s in range(secs)], [])
    second = sum([down(s) if s % 2 == 0 else up(s) for s in range(secs)], [])
    got_first = lax.ppermute(block, ("sec", "col"), first)
    got_second = lax.ppermute(block, ("sec", "col"), second)
    even = lax.axis_index("sec") % 2 == 0
    low = jnp.where(even, got_first, got_second)
    high = jnp.where(even, got_second, got_first)
    return low, high


def local(velocity, thrust, band_counts, farm_split, turbine_cells):
    moving_bf = velocity[0]
    rows_here = moving_bf.shape[2]
    count_z = moving_bf.shape[3]
    col_index = lax.axis_index("col")
    cols = lax.axis_size("col")
    span_total = rows_here * cols
    farm_on = (lax.axis_index("sec") == 1).astype(jnp.float32)
    modes_np = slot_modes()
    deriv_bf, cas_x = lax.optimization_barrier(
        (deriv_table(), jnp.asarray(cas_table(modes_np, NX).astype(np.float32)))
    )

    low, high = halo(moving_bf, cols)
    outflow = lax.ppermute(moving_bf[:, NX - FR :], "sec", [(0, 1)])

    moving = moving_bf.astype(jnp.float32)
    along_x = jnp.einsum("ij,cjyz->ciyz", deriv_bf, moving_bf, preferred_element_type=jnp.float32)
    along_y = (high.astype(jnp.float32) - low.astype(jnp.float32)) * 0.5
    along_z = zdiff(moving)
    advection = moving[0] * along_x + moving[1] * along_y + moving[2] * along_z
    weights = fringe_weights(farm_split[0]) * farm_on
    target = jnp.einsum("xj,cjyz->cxyz", weights, outflow.astype(jnp.float32), precision=highest)
    fringe = target - jnp.sum(weights, axis=1)[None, :, None, None] * moving
    ycoord = col_index * rows_here + jnp.arange(rows_here, dtype=jnp.int32)
    drag_field = turbine_field(turbine_cells, thrust, ycoord, count_z, span_total) * farm_on
    thrust_force = -0.5 * drag_field * moving[0] * jnp.abs(moving[0])
    tendency = -advection + fringe
    tendency = jnp.concatenate([tendency[:1] + thrust_force[None], tendency[1:]], axis=0)
    ustar = (moving + time_step * tendency).astype(jnp.bfloat16)
    side_low, side_high = halo(ustar[1], cols)
    side_low = side_low.astype(jnp.float32)
    side_high = side_high.astype(jnp.float32)
    ustar_f = ustar.astype(jnp.float32)
    divergence = jnp.einsum("ij,jyz->iyz", deriv_bf, ustar[0], preferred_element_type=jnp.float32)
    divergence = divergence + (side_high - side_low) * 0.5
    divergence = divergence + zdiff(ustar_f[2])
    source = divergence / time_step
    modes = jnp.asarray(modes_np.astype(np.int32))
    retained = kept_mask(modes, band_counts[0])
    spec = jnp.einsum("kx,xyz->kyz", cas_x, source, precision=lax.Precision.HIGH) * retained[:, None, None]
    columns = lax.all_to_all(spec, "col", split_axis=0, concat_axis=1, tiled=True)
    per_device = columns.shape[0]
    local_modes = lax.dynamic_slice_in_dim(modes, col_index * per_device, per_device)
    solved = column_solve(columns, local_modes)
    back = lax.all_to_all(solved, "col", split_axis=2, concat_axis=0, tiled=True)
    pres_modes = back[:, 0]
    grad_modes = back[:, 1]
    signed = np.where(modes_np < NX // 2, modes_np, modes_np - NX).astype(np.float32)
    mirrored = jnp.concatenate([pres_modes[:1], jnp.flip(pres_modes[1:], axis=0)], axis=0)
    dx_modes = -jnp.asarray(signed)[:, None, None] * mirrored
    stacked = jnp.stack([pres_modes, dx_modes, grad_modes], axis=0)
    fields = jnp.einsum("kx,gkyz->gxyz", cas_x, stacked, precision=lax.Precision.HIGH) / NX
    pressure = fields[0]
    grad_x = fields[1]
    grad_y = fields[2]
    grad_z = zdiff(pressure)
    newer = ustar_f - time_step * jnp.stack([grad_x, grad_y, grad_z], axis=0)
    return (newer.astype(jnp.bfloat16)[None], pressure[None])


def solution(mesh):
    return jax.shard_map(
        local,
        mesh=mesh,
        in_specs=(P("sec", None, None, "col", None), P(), P("sec", None), P(), P()),
        out_specs=(P("sec", None, None, "col", None), P("sec", None, "col", None)),
        check_vma=False,
    )
```

```python
import numpy as np
import jax
import jax.numpy as jnp
from jax import lax
from jax.sharding import PartitionSpec as P

NX = 1024
BAND = 32
NB = 10
FR = 32
DISK = 4
KX = 320
SLOTS = 2 * KX


highest = lax.Precision.HIGHEST
time_step = 0.25
screen = 0.01
fringe_rate = 2.0


def slot_modes():
    slots = np.arange(SLOTS)
    return np.where(slots < KX, slots, slots + NX - SLOTS)


def deriv_table():
    index = np.arange(NX)
    offset = (index[:, None] - index[None, :]) % NX
    angle = np.pi * offset / NX
    parity = 1.0 - 2.0 * (offset % 2)
    denom = np.where(offset == 0, 1.0, np.sin(angle))
    table = np.where(offset == 0, 0.0, 0.5 * parity * np.cos(angle) / denom)
    return jnp.asarray(table.astype(np.float32)).astype(jnp.bfloat16)


def cas_table(modes, length):
    cells = np.arange(length)
    angle = 2.0 * np.pi * ((modes[:, None] * cells[None, :]) % length) / length
    return np.cos(angle) + np.sin(angle)


def cosine_np(length):
    index = np.arange(length)
    angle = np.pi * index[:, None] * (2 * index[None, :] + 1) / (2 * length)
    scale = np.where(index == 0, np.sqrt(1.0 / length), np.sqrt(2.0 / length))
    return np.cos(angle) * scale[:, None]


def signed_np(length):
    index = np.arange(length)
    return np.where(index < length // 2, index, np.where(index > length // 2, index - length, 0))


def wave_square(mode_ids, length):
    folded = jnp.minimum(mode_ids, length - mode_ids).astype(jnp.float32)
    return (2.0 * jnp.pi * folded / length) ** 2


def kept_mask(mode_ids, counts):
    folded = jnp.minimum(mode_ids, NX - mode_ids)
    band_of = folded // BAND
    onehot = band_of[:, None] == jnp.arange(NB, dtype=jnp.int32)[None, :]
    limit_per = jnp.sum(jnp.where(onehot, counts[None, :], 0), axis=1)
    return ((folded < KX) & (folded % BAND < limit_per)).astype(jnp.float32)


def zdiff(field):
    zeros = jnp.zeros(field.shape[:-1] + (1,), jnp.float32)
    upper = jnp.concatenate([field[..., 1:], zeros], axis=-1)
    lower = jnp.concatenate([zeros, field[..., :-1]], axis=-1)
    return (upper - lower) * 0.5


def fringe_weights(split_at):
    cells = jnp.arange(NX, dtype=jnp.int32)[:, None]
    plane = jnp.arange(FR, dtype=jnp.int32)[None, :]
    rate = fringe_rate * jnp.sin(jnp.pi * (plane.astype(jnp.float32) + 0.5) / FR) ** 2
    inside = (cells == plane) | (cells == split_at + plane)
    return jnp.where(inside, rate, 0.0)


def turbine_field(cells, thrust, ycoord, count_z, span_total):
    onehot_x = (cells[:, 0][:, None] == jnp.arange(NX, dtype=jnp.int32)[None, :]).astype(
        jnp.float32
    ) * thrust[:, None]
    offset_y = (ycoord[None, :] - cells[:, 1][:, None]) % span_total
    onehot_y = ((offset_y <= DISK) | (offset_y >= span_total - DISK)).astype(jnp.float32)
    offset_z = jnp.abs(jnp.arange(count_z, dtype=jnp.int32)[None, :] - cells[:, 2][:, None])
    onehot_z = (offset_z <= DISK).astype(jnp.float32)
    cross_yz = (onehot_y[:, :, None] * onehot_z[:, None, :]).reshape(cells.shape[0], -1)
    field = jnp.dot(onehot_x.T, cross_yz, precision=highest)
    return field.reshape(NX, ycoord.shape[0], count_z)


def column_solve(columns, local_modes):
    cells_y = columns.shape[1]
    cells_z = columns.shape[2]
    ids_y = np.arange(cells_y)
    cas_y = jnp.asarray(cas_table(ids_y, cells_y).astype(np.float32))
    cos_z = jnp.asarray(cosine_np(cells_z).astype(np.float32))
    wave_y = 2.0 * np.pi * signed_np(cells_y) / cells_y
    back_p = cas_table(ids_y, cells_y) / cells_y
    back_g = wave_y[:, None] * cas_table((-ids_y) % cells_y, cells_y) / cells_y
    back_y = jnp.asarray(np.stack([back_p, back_g]).astype(np.float32))
    first = jnp.einsum("jy,ryz->rjz", cas_y, columns, precision=lax.Precision.HIGH)
    second = jnp.einsum("rjz,mz->rjm", first, cos_z, precision=lax.Precision.HIGH)
    kz_sq = (jnp.pi * jnp.arange(cells_z, dtype=jnp.int32).astype(jnp.float32) / cells_z) ** 2
    eigen = (
        wave_square(local_modes, NX)[:, None, None]
        + wave_square(jnp.arange(cells_y, dtype=jnp.int32), cells_y)[None, :, None]
        + kz_sq[None, None, :]
        + screen
    )
    p_hat = -second / eigen
    back = jnp.einsum("gjy,rjm->rgym", back_y, p_hat, precision=lax.Precision.HIGH)
    return jnp.einsum("rgym,mz->rgyz", back, cos_z, precision=lax.Precision.HIGH)


def halo(block, cols):
    secs = lax.axis_size("sec")
    up = lambda s: [(s * cols + i, s * cols + (i + 1) % cols) for i in range(cols)]
    down = lambda s: [(s * cols + (i + 1) % cols, s * cols + i) for i in range(cols)]
    first = sum([up(s) if s % 2 == 0 else down(s) for s in range(secs)], [])
    second = sum([down(s) if s % 2 == 0 else up(s) for s in range(secs)], [])
    got_first = lax.ppermute(block, ("sec", "col"), first)
    got_second = lax.ppermute(block, ("sec", "col"), second)
    even = lax.axis_index("sec") % 2 == 0
    low = jnp.where(even, got_first, got_second)
    high = jnp.where(even, got_second, got_first)
    return low, high


def local(velocity, thrust, band_counts, farm_split, turbine_cells):
    moving_bf = velocity[0]
    rows_here = moving_bf.shape[2]
    count_z = moving_bf.shape[3]
    col_index = lax.axis_index("col")
    cols = lax.axis_size("col")
    span_total = rows_here * cols
    farm_on = (lax.axis_index("sec") == 1).astype(jnp.float32)
    deriv_bf = deriv_table()
    modes_np = slot_modes()
    cas_x = jnp.asarray(cas_table(modes_np, NX).astype(np.float32))

    low, high = halo(moving_bf, cols)
    outflow = lax.ppermute(moving_bf[:, NX - FR :], "sec", [(0, 1)])

    moving = moving_bf.astype(jnp.float32)
    along_x = jnp.einsum("ij,cjyz->ciyz", deriv_bf, moving_bf, preferred_element_type=jnp.float32)
    along_y = (high.astype(jnp.float32) - low.astype(jnp.float32)) * 0.5
    along_z = zdiff(moving)
    advection = moving[0] * along_x + moving[1] * along_y + moving[2] * along_z
    weights = fringe_weights(farm_split[0]) * farm_on
    target = jnp.einsum("xj,cjyz->cxyz", weights, outflow.astype(jnp.float32), precision=highest)
    fringe = target - jnp.sum(weights, axis=1)[None, :, None, None] * moving
    ycoord = col_index * rows_here + jnp.arange(rows_here, dtype=jnp.int32)
    drag_field = turbine_field(turbine_cells, thrust, ycoord, count_z, span_total) * farm_on
    thrust_force = -0.5 * drag_field * moving[0] * jnp.abs(moving[0])
    tendency = -advection + fringe
    tendency = jnp.concatenate([tendency[:1] + thrust_force[None], tendency[1:]], axis=0)
    ustar = (moving + time_step * tendency).astype(jnp.bfloat16)
    side_low, side_high = halo(ustar[1], cols)
    side_low = side_low.astype(jnp.float32)
    side_high = side_high.astype(jnp.float32)
    ustar_f = ustar.astype(jnp.float32)
    divergence = jnp.einsum("ij,jyz->iyz", deriv_bf, ustar[0], preferred_element_type=jnp.float32)
    divergence = divergence + (side_high - side_low) * 0.5
    divergence = divergence + zdiff(ustar_f[2])
    source = divergence / time_step
    modes = jnp.asarray(modes_np.astype(np.int32))
    retained = kept_mask(modes, band_counts[0])
    spec = jnp.einsum("kx,xyz->kyz", cas_x, source, precision=lax.Precision.HIGH) * retained[:, None, None]
    columns = lax.all_to_all(spec, "col", split_axis=0, concat_axis=1, tiled=True)
    per_device = columns.shape[0]
    local_modes = lax.dynamic_slice_in_dim(modes, col_index * per_device, per_device)
    solved = column_solve(columns, local_modes)
    back = lax.all_to_all(solved, "col", split_axis=2, concat_axis=0, tiled=True)
    pres_modes = back[:, 0]
    grad_modes = back[:, 1]
    signed = np.where(modes_np < NX // 2, modes_np, modes_np - NX).astype(np.float32)
    mirrored = jnp.concatenate([pres_modes[:1], jnp.flip(pres_modes[1:], axis=0)], axis=0)
    dx_modes = -jnp.asarray(signed)[:, None, None] * mirrored
    stacked = jnp.stack([pres_modes, dx_modes, grad_modes], axis=0)
    fields = jnp.einsum("kx,gkyz->gxyz", cas_x, stacked, precision=lax.Precision.HIGH) / NX
    pressure = fields[0]
    grad_x = fields[1]
    grad_y = fields[2]
    grad_z = zdiff(pressure)
    newer = ustar_f - time_step * jnp.stack([grad_x, grad_y, grad_z], axis=0)
    return (newer.astype(jnp.bfloat16)[None], pressure[None])


def solution(mesh):
    return jax.shard_map(
        local,
        mesh=mesh,
        in_specs=(P("sec", None, None, "col", None), P(), P("sec", None), P(), P()),
        out_specs=(P("sec", None, None, "col", None), P("sec", None, "col", None)),
        check_vma=False,
    )
```

```python
import numpy as np
import jax
import jax.numpy as jnp
from jax import lax
from jax.sharding import PartitionSpec as P

NX = 1024
BAND = 32
NB = 10
FR = 32
DISK = 4
KX = 320
SLOTS = 2 * KX


highest = lax.Precision.HIGHEST
time_step = 0.25
screen = 0.01
fringe_rate = 2.0


def slot_modes():
    slots = np.arange(SLOTS)
    return np.where(slots < KX, slots, slots + NX - SLOTS)


def deriv_table():
    index = np.arange(NX)
    offset = (index[:, None] - index[None, :]) % NX
    angle = np.pi * offset / NX
    parity = 1.0 - 2.0 * (offset % 2)
    denom = np.where(offset == 0, 1.0, np.sin(angle))
    table = np.where(offset == 0, 0.0, 0.5 * parity * np.cos(angle) / denom)
    return jnp.asarray(table.astype(np.float32)).astype(jnp.bfloat16)


def cas_table(modes, length):
    cells = np.arange(length)
    angle = 2.0 * np.pi * ((modes[:, None] * cells[None, :]) % length) / length
    return np.cos(angle) + np.sin(angle)


def cosine_np(length):
    index = np.arange(length)
    angle = np.pi * index[:, None] * (2 * index[None, :] + 1) / (2 * length)
    scale = np.where(index == 0, np.sqrt(1.0 / length), np.sqrt(2.0 / length))
    return np.cos(angle) * scale[:, None]


def signed_np(length):
    index = np.arange(length)
    return np.where(index < length // 2, index, np.where(index > length // 2, index - length, 0))


def wave_square(mode_ids, length):
    folded = jnp.minimum(mode_ids, length - mode_ids).astype(jnp.float32)
    return (2.0 * jnp.pi * folded / length) ** 2


def kept_mask(mode_ids, counts):
    folded = jnp.minimum(mode_ids, NX - mode_ids)
    band_of = folded // BAND
    onehot = band_of[:, None] == jnp.arange(NB, dtype=jnp.int32)[None, :]
    limit_per = jnp.sum(jnp.where(onehot, counts[None, :], 0), axis=1)
    return ((folded < KX) & (folded % BAND < limit_per)).astype(jnp.float32)


def zdiff(field):
    zeros = jnp.zeros(field.shape[:-1] + (1,), jnp.float32)
    upper = jnp.concatenate([field[..., 1:], zeros], axis=-1)
    lower = jnp.concatenate([zeros, field[..., :-1]], axis=-1)
    return (upper - lower) * 0.5


def fringe_weights(split_at):
    cells = jnp.arange(NX, dtype=jnp.int32)[:, None]
    plane = jnp.arange(FR, dtype=jnp.int32)[None, :]
    rate = fringe_rate * jnp.sin(jnp.pi * (plane.astype(jnp.float32) + 0.5) / FR) ** 2
    inside = (cells == plane) | (cells == split_at + plane)
    return jnp.where(inside, rate, 0.0)


def turbine_field(cells, thrust, ycoord, count_z, span_total):
    onehot_x = (cells[:, 0][:, None] == jnp.arange(NX, dtype=jnp.int32)[None, :]).astype(
        jnp.float32
    ) * thrust[:, None]
    offset_y = (ycoord[None, :] - cells[:, 1][:, None]) % span_total
    onehot_y = ((offset_y <= DISK) | (offset_y >= span_total - DISK)).astype(jnp.float32)
    offset_z = jnp.abs(jnp.arange(count_z, dtype=jnp.int32)[None, :] - cells[:, 2][:, None])
    onehot_z = (offset_z <= DISK).astype(jnp.float32)
    cross_yz = (onehot_y[:, :, None] * onehot_z[:, None, :]).reshape(cells.shape[0], -1)
    field = jnp.dot(onehot_x.T, cross_yz, precision=highest)
    return field.reshape(NX, ycoord.shape[0], count_z)


def column_solve(columns, local_modes):
    cells_y = columns.shape[1]
    cells_z = columns.shape[2]
    ids_y = np.arange(cells_y)
    cas_y = jnp.asarray(cas_table(ids_y, cells_y).astype(np.float32))
    cos_z = jnp.asarray(cosine_np(cells_z).astype(np.float32))
    wave_y = 2.0 * np.pi * signed_np(cells_y) / cells_y
    back_p = cas_table(ids_y, cells_y) / cells_y
    back_g = wave_y[:, None] * cas_table((-ids_y) % cells_y, cells_y) / cells_y
    back_y = jnp.asarray(np.stack([back_p, back_g]).astype(np.float32))
    first = jnp.einsum("jy,ryz->rjz", cas_y, columns, precision=lax.Precision.HIGH)
    second = jnp.einsum("rjz,mz->rjm", first, cos_z, precision=lax.Precision.HIGH)
    kz_sq = (jnp.pi * jnp.arange(cells_z, dtype=jnp.int32).astype(jnp.float32) / cells_z) ** 2
    eigen = (
        wave_square(local_modes, NX)[:, None, None]
        + wave_square(jnp.arange(cells_y, dtype=jnp.int32), cells_y)[None, :, None]
        + kz_sq[None, None, :]
        + screen
    )
    p_hat = -second / eigen
    back = jnp.einsum("gjy,rjm->rgym", back_y, p_hat, precision=lax.Precision.HIGH)
    return jnp.einsum("rgym,mz->rgyz", back, cos_z, precision=lax.Precision.HIGH)


def halo(block, cols):
    secs = lax.axis_size("sec")
    up = lambda s: [(s * cols + i, s * cols + (i + 1) % cols) for i in range(cols)]
    down = lambda s: [(s * cols + (i + 1) % cols, s * cols + i) for i in range(cols)]
    first = sum([up(s) if s % 2 == 0 else down(s) for s in range(secs)], [])
    second = sum([down(s) if s % 2 == 0 else up(s) for s in range(secs)], [])
    got_first = lax.ppermute(block, ("sec", "col"), first)
    got_second = lax.ppermute(block, ("sec", "col"), second)
    even = lax.axis_index("sec") % 2 == 0
    low = jnp.where(even, got_first, got_second)
    high = jnp.where(even, got_second, got_first)
    return low, high


def local(velocity, thrust, band_counts, farm_split, turbine_cells):
    moving_bf = velocity[0]
    rows_here = moving_bf.shape[2]
    count_z = moving_bf.shape[3]
    col_index = lax.axis_index("col")
    cols = lax.axis_size("col")
    span_total = rows_here * cols
    farm_on = (lax.axis_index("sec") == 1).astype(jnp.float32)
    deriv_bf = deriv_table()
    modes_np = slot_modes()
    cas_x = jnp.asarray(cas_table(modes_np, NX).astype(np.float32))

    low, high = halo(moving_bf, cols)
    low2 = lax.ppermute(moving_bf[1], "col", [(i, (i + 2) % cols) for i in range(cols)])
    high2 = lax.ppermute(moving_bf[1], "col", [((i + 2) % cols, i) for i in range(cols)])
    outflow = lax.ppermute(moving_bf[:, NX - FR :], "sec", [(0, 1)])
    slab_one = moving_bf[1, NX - FR :]
    slab_low = lax.ppermute(slab_one, ("sec", "col"), [(c, cols + (c + 1) % cols) for c in range(cols)])
    slab_high = lax.ppermute(slab_one, ("sec", "col"), [(c, cols + (c - 1) % cols) for c in range(cols)])

    moving = moving_bf.astype(jnp.float32)
    rows_in = jnp.concatenate([moving_bf, low[1:2], high[1:2]], axis=0)
    along_all = jnp.einsum("ij,cjyz->ciyz", deriv_bf, rows_in, preferred_element_type=jnp.float32)
    along_x = along_all[:3]
    along_y = (high.astype(jnp.float32) - low.astype(jnp.float32)) * 0.5
    along_z = zdiff(moving)
    advection = moving[0] * along_x + moving[1] * along_y + moving[2] * along_z
    weights = fringe_weights(farm_split[0]) * farm_on
    target = jnp.einsum("xj,cjyz->cxyz", weights, outflow.astype(jnp.float32), precision=highest)
    fringe = target - jnp.sum(weights, axis=1)[None, :, None, None] * moving
    ycoord = col_index * rows_here + jnp.arange(rows_here, dtype=jnp.int32)
    drag_field = turbine_field(turbine_cells, thrust, ycoord, count_z, span_total) * farm_on
    thrust_force = -0.5 * drag_field * moving[0] * jnp.abs(moving[0])
    tendency = -advection + fringe
    tendency = jnp.concatenate([tendency[:1] + thrust_force[None], tendency[1:]], axis=0)
    ustar = (moving + time_step * tendency).astype(jnp.bfloat16)
    wsum = jnp.sum(weights, axis=1)[:, None, None]

    def side_ustar(row, ax_one, below, above, slab):
        row_f = row.astype(jnp.float32)
        ay_one = (above.astype(jnp.float32) - below.astype(jnp.float32)) * 0.5
        adv = row_f[0] * ax_one + row_f[1] * ay_one + row_f[2] * zdiff(row_f[1])
        tgt = jnp.einsum("xj,jyz->xyz", weights, slab.astype(jnp.float32), precision=highest)
        ten = -adv + (tgt - wsum * row_f[1])
        return (row_f[1] + time_step * ten).astype(jnp.bfloat16).astype(jnp.float32)

    side_low = side_ustar(low, along_all[3], low2, moving_bf[1], slab_low)
    side_high = side_ustar(high, along_all[4], moving_bf[1], high2, slab_high)
    ustar_f = ustar.astype(jnp.float32)
    divergence = jnp.einsum("ij,jyz->iyz", deriv_bf, ustar[0], preferred_element_type=jnp.float32)
    divergence = divergence + (side_high - side_low) * 0.5
    divergence = divergence + zdiff(ustar_f[2])
    source = divergence / time_step
    modes = jnp.asarray(modes_np.astype(np.int32))
    retained = kept_mask(modes, band_counts[0])
    spec = jnp.einsum("kx,xyz->kyz", cas_x, source, precision=lax.Precision.HIGH) * retained[:, None, None]
    columns = lax.all_to_all(spec, "col", split_axis=0, concat_axis=1, tiled=True)
    per_device = columns.shape[0]
    local_modes = lax.dynamic_slice_in_dim(modes, col_index * per_device, per_device)
    solved = column_solve(columns, local_modes)
    back = lax.all_to_all(solved, "col", split_axis=2, concat_axis=0, tiled=True)
    pres_modes = back[:, 0]
    grad_modes = back[:, 1]
    signed = np.where(modes_np < NX // 2, modes_np, modes_np - NX).astype(np.float32)
    mirrored = jnp.concatenate([pres_modes[:1], jnp.flip(pres_modes[1:], axis=0)], axis=0)
    dx_modes = -jnp.asarray(signed)[:, None, None] * mirrored
    stacked = jnp.stack([pres_modes, dx_modes, grad_modes], axis=0)
    fields = jnp.einsum("kx,gkyz->gxyz", cas_x, stacked, precision=lax.Precision.HIGH) / NX
    pressure = fields[0]
    grad_x = fields[1]
    grad_y = fields[2]
    grad_z = zdiff(pressure)
    newer = ustar_f - time_step * jnp.stack([grad_x, grad_y, grad_z], axis=0)
    return (newer.astype(jnp.bfloat16)[None], pressure[None])


def solution(mesh):
    return jax.shard_map(
        local,
        mesh=mesh,
        in_specs=(P("sec", None, None, "col", None), P(), P("sec", None), P(), P()),
        out_specs=(P("sec", None, None, "col", None), P("sec", None, "col", None)),
        check_vma=False,
    )
```

```python
import numpy as np
import jax
import jax.numpy as jnp
from jax import lax
from jax.sharding import PartitionSpec as P

NX = 1024
BAND = 32
NB = 10
FR = 32
DISK = 4
KX = 320
SLOTS = 2 * KX


highest = lax.Precision.HIGHEST
time_step = 0.25
screen = 0.01
fringe_rate = 2.0


def slot_modes():
    slots = np.arange(SLOTS)
    return np.where(slots < KX, slots, slots + NX - SLOTS)


def deriv_table():
    index = np.arange(NX)
    offset = (index[:, None] - index[None, :]) % NX
    angle = np.pi * offset / NX
    parity = 1.0 - 2.0 * (offset % 2)
    denom = np.where(offset == 0, 1.0, np.sin(angle))
    table = np.where(offset == 0, 0.0, 0.5 * parity * np.cos(angle) / denom)
    return jnp.asarray(table.astype(np.float32)).astype(jnp.bfloat16)


def cas_table(modes, length):
    cells = np.arange(length)
    angle = 2.0 * np.pi * ((modes[:, None] * cells[None, :]) % length) / length
    return np.cos(angle) + np.sin(angle)


def cosine_np(length):
    index = np.arange(length)
    angle = np.pi * index[:, None] * (2 * index[None, :] + 1) / (2 * length)
    scale = np.where(index == 0, np.sqrt(1.0 / length), np.sqrt(2.0 / length))
    return np.cos(angle) * scale[:, None]


def signed_np(length):
    index = np.arange(length)
    return np.where(index < length // 2, index, np.where(index > length // 2, index - length, 0))


def wave_square(mode_ids, length):
    folded = jnp.minimum(mode_ids, length - mode_ids).astype(jnp.float32)
    return (2.0 * jnp.pi * folded / length) ** 2


def kept_mask(mode_ids, counts):
    folded = jnp.minimum(mode_ids, NX - mode_ids)
    band_of = folded // BAND
    onehot = band_of[:, None] == jnp.arange(NB, dtype=jnp.int32)[None, :]
    limit_per = jnp.sum(jnp.where(onehot, counts[None, :], 0), axis=1)
    return ((folded < KX) & (folded % BAND < limit_per)).astype(jnp.float32)


def zdiff(field):
    zeros = jnp.zeros(field.shape[:-1] + (1,), jnp.float32)
    upper = jnp.concatenate([field[..., 1:], zeros], axis=-1)
    lower = jnp.concatenate([zeros, field[..., :-1]], axis=-1)
    return (upper - lower) * 0.5


def fringe_weights(split_at):
    cells = jnp.arange(NX, dtype=jnp.int32)[:, None]
    plane = jnp.arange(FR, dtype=jnp.int32)[None, :]
    rate = fringe_rate * jnp.sin(jnp.pi * (plane.astype(jnp.float32) + 0.5) / FR) ** 2
    inside = (cells == plane) | (cells == split_at + plane)
    return jnp.where(inside, rate, 0.0)


def turbine_field(cells, thrust, ycoord, count_z, span_total):
    onehot_x = (cells[:, 0][:, None] == jnp.arange(NX, dtype=jnp.int32)[None, :]).astype(
        jnp.float32
    ) * thrust[:, None]
    offset_y = (ycoord[None, :] - cells[:, 1][:, None]) % span_total
    onehot_y = ((offset_y <= DISK) | (offset_y >= span_total - DISK)).astype(jnp.float32)
    offset_z = jnp.abs(jnp.arange(count_z, dtype=jnp.int32)[None, :] - cells[:, 2][:, None])
    onehot_z = (offset_z <= DISK).astype(jnp.float32)
    cross_yz = (onehot_y[:, :, None] * onehot_z[:, None, :]).reshape(cells.shape[0], -1)
    field = jnp.dot(onehot_x.T, cross_yz, precision=highest)
    return field.reshape(NX, ycoord.shape[0], count_z)


def column_solve(columns, local_modes):
    cells_y = columns.shape[1]
    cells_z = columns.shape[2]
    ids_y = np.arange(cells_y)
    cas_y = jnp.asarray(cas_table(ids_y, cells_y).astype(np.float32))
    cos_z = jnp.asarray(cosine_np(cells_z).astype(np.float32))
    wave_y = 2.0 * np.pi * signed_np(cells_y) / cells_y
    back_p = cas_table(ids_y, cells_y) / cells_y
    back_g = wave_y[:, None] * cas_table((-ids_y) % cells_y, cells_y) / cells_y
    back_y = jnp.asarray(np.stack([back_p, back_g]).astype(np.float32))
    first = jnp.einsum("jy,ryz->rjz", cas_y, columns, precision=lax.Precision.HIGH)
    second = jnp.einsum("rjz,mz->rjm", first, cos_z, precision=lax.Precision.HIGH)
    kz_sq = (jnp.pi * jnp.arange(cells_z, dtype=jnp.int32).astype(jnp.float32) / cells_z) ** 2
    eigen = (
        wave_square(local_modes, NX)[:, None, None]
        + wave_square(jnp.arange(cells_y, dtype=jnp.int32), cells_y)[None, :, None]
        + kz_sq[None, None, :]
        + screen
    )
    p_hat = -second / eigen
    back = jnp.einsum("gjy,rjm->rgym", back_y, p_hat, precision=lax.Precision.HIGH)
    return jnp.einsum("rgym,mz->rgyz", back, cos_z, precision=lax.Precision.HIGH)


def halo(block, cols):
    secs = lax.axis_size("sec")
    up = lambda s: [(s * cols + i, s * cols + (i + 1) % cols) for i in range(cols)]
    down = lambda s: [(s * cols + (i + 1) % cols, s * cols + i) for i in range(cols)]
    first = sum([up(s) if s % 2 == 0 else down(s) for s in range(secs)], [])
    second = sum([down(s) if s % 2 == 0 else up(s) for s in range(secs)], [])
    got_first = lax.ppermute(block, ("sec", "col"), first)
    got_second = lax.ppermute(block, ("sec", "col"), second)
    even = lax.axis_index("sec") % 2 == 0
    low = jnp.where(even, got_first, got_second)
    high = jnp.where(even, got_second, got_first)
    return low, high


def local(velocity, thrust, band_counts, farm_split, turbine_cells):
    moving_bf = velocity[0]
    rows_here = moving_bf.shape[2]
    count_z = moving_bf.shape[3]
    col_index = lax.axis_index("col")
    cols = lax.axis_size("col")
    span_total = rows_here * cols
    farm_on = (lax.axis_index("sec") == 1).astype(jnp.float32)
    deriv_bf = deriv_table()
    modes_np = slot_modes()
    cas_x = jnp.asarray(cas_table(modes_np, NX).astype(np.float32))

    low, high = halo(moving_bf, cols)
    outflow = lax.ppermute(moving_bf[:, NX - FR :], "sec", [(0, 1)])

    moving = moving_bf.astype(jnp.float32)
    along_x = jnp.einsum("ij,cjyz->ciyz", deriv_bf, moving_bf, preferred_element_type=jnp.float32)
    along_y = (high.astype(jnp.float32) - low.astype(jnp.float32)) * 0.5
    along_z = zdiff(moving)
    advection = moving[0] * along_x + moving[1] * along_y + moving[2] * along_z
    weights = fringe_weights(farm_split[0]) * farm_on
    target = jnp.einsum("xj,cjyz->cxyz", weights, outflow.astype(jnp.float32), precision=highest)
    fringe = target - jnp.sum(weights, axis=1)[None, :, None, None] * moving
    ycoord = col_index * rows_here + jnp.arange(rows_here, dtype=jnp.int32)
    drag_field = turbine_field(turbine_cells, thrust, ycoord, count_z, span_total) * farm_on
    thrust_force = -0.5 * drag_field * moving[0] * jnp.abs(moving[0])
    tendency = -advection + fringe
    tendency = jnp.concatenate([tendency[:1] + thrust_force[None], tendency[1:]], axis=0)
    ustar = (moving + time_step * tendency).astype(jnp.bfloat16)
    side_low, side_high = halo(ustar[1], cols)
    side_low = side_low.astype(jnp.float32)
    side_high = side_high.astype(jnp.float32)
    ustar_f = ustar.astype(jnp.float32)
    divergence = jnp.einsum("ij,jyz->iyz", deriv_bf, ustar[0], preferred_element_type=jnp.float32)
    divergence = divergence + (side_high - side_low) * 0.5
    divergence = divergence + zdiff(ustar_f[2])
    source = divergence / time_step
    modes = jnp.asarray(modes_np.astype(np.int32))
    retained = kept_mask(modes, band_counts[0])
    spec = jnp.einsum("kx,xyz->kyz", cas_x, source, precision=lax.Precision.HIGH) * retained[:, None, None]
    depth = spec.shape[-1]
    columns = lax.all_to_all(spec.reshape(cols, -1), "col", split_axis=0, concat_axis=0, tiled=True)
    columns = columns.reshape(cols, -1, depth).transpose(1, 0, 2)
    per_device = columns.shape[0]
    local_modes = lax.dynamic_slice_in_dim(modes, col_index * per_device, per_device)
    solved = column_solve(columns, local_modes)
    back = lax.all_to_all(solved.transpose(2, 0, 1, 3), "col", split_axis=0, concat_axis=0, tiled=True)
    back = back.reshape(-1, 2, back.shape[-1])
    pres_modes = back[:, 0][:, None]
    grad_modes = back[:, 1][:, None]
    signed = np.where(modes_np < NX // 2, modes_np, modes_np - NX).astype(np.float32)
    mirrored = jnp.concatenate([pres_modes[:1], jnp.flip(pres_modes[1:], axis=0)], axis=0)
    dx_modes = -jnp.asarray(signed)[:, None, None] * mirrored
    stacked = jnp.stack([pres_modes, dx_modes, grad_modes], axis=0)
    fields = jnp.einsum("kx,gkyz->gxyz", cas_x, stacked, precision=lax.Precision.HIGH) / NX
    pressure = fields[0]
    grad_x = fields[1]
    grad_y = fields[2]
    grad_z = zdiff(pressure)
    newer = ustar_f - time_step * jnp.stack([grad_x, grad_y, grad_z], axis=0)
    return (newer.astype(jnp.bfloat16)[None], pressure[None])


def solution(mesh):
    return jax.shard_map(
        local,
        mesh=mesh,
        in_specs=(P("sec", None, None, "col", None), P(), P("sec", None), P(), P()),
        out_specs=(P("sec", None, None, "col", None), P("sec", None, "col", None)),
        check_vma=False,
    )
```

```python
import numpy as np
import jax
import jax.numpy as jnp
from jax import lax
from jax.sharding import PartitionSpec as P

NX = 1024
BAND = 32
NB = 10
FR = 32
DISK = 4
KX = 320
SLOTS = 2 * KX


highest = lax.Precision.HIGHEST
time_step = 0.25
screen = 0.01
fringe_rate = 2.0


def slot_modes():
    slots = np.arange(SLOTS)
    return np.where(slots < KX, slots, slots + NX - SLOTS)


def deriv_table():
    index = np.arange(NX)
    offset = (index[:, None] - index[None, :]) % NX
    angle = np.pi * offset / NX
    parity = 1.0 - 2.0 * (offset % 2)
    denom = np.where(offset == 0, 1.0, np.sin(angle))
    table = np.where(offset == 0, 0.0, 0.5 * parity * np.cos(angle) / denom)
    return jnp.asarray(table.astype(np.float32)).astype(jnp.bfloat16)


def cas_table(modes, length):
    cells = np.arange(length)
    angle = 2.0 * np.pi * ((modes[:, None] * cells[None, :]) % length) / length
    return np.cos(angle) + np.sin(angle)


def cosine_np(length):
    index = np.arange(length)
    angle = np.pi * index[:, None] * (2 * index[None, :] + 1) / (2 * length)
    scale = np.where(index == 0, np.sqrt(1.0 / length), np.sqrt(2.0 / length))
    return np.cos(angle) * scale[:, None]


def signed_np(length):
    index = np.arange(length)
    return np.where(index < length // 2, index, np.where(index > length // 2, index - length, 0))


def wave_square(mode_ids, length):
    folded = jnp.minimum(mode_ids, length - mode_ids).astype(jnp.float32)
    return (2.0 * jnp.pi * folded / length) ** 2


def kept_mask(mode_ids, counts):
    folded = jnp.minimum(mode_ids, NX - mode_ids)
    band_of = folded // BAND
    onehot = band_of[:, None] == jnp.arange(NB, dtype=jnp.int32)[None, :]
    limit_per = jnp.sum(jnp.where(onehot, counts[None, :], 0), axis=1)
    return ((folded < KX) & (folded % BAND < limit_per)).astype(jnp.float32)


def zdiff(field):
    zeros = jnp.zeros(field.shape[:-1] + (1,), jnp.float32)
    upper = jnp.concatenate([field[..., 1:], zeros], axis=-1)
    lower = jnp.concatenate([zeros, field[..., :-1]], axis=-1)
    return (upper - lower) * 0.5


def fringe_weights(split_at):
    cells = jnp.arange(NX, dtype=jnp.int32)[:, None]
    plane = jnp.arange(FR, dtype=jnp.int32)[None, :]
    rate = fringe_rate * jnp.sin(jnp.pi * (plane.astype(jnp.float32) + 0.5) / FR) ** 2
    inside = (cells == plane) | (cells == split_at + plane)
    return jnp.where(inside, rate, 0.0)


def turbine_field(cells, thrust, ycoord, count_z, span_total):
    onehot_x = (cells[:, 0][:, None] == jnp.arange(NX, dtype=jnp.int32)[None, :]).astype(
        jnp.float32
    ) * thrust[:, None]
    offset_y = (ycoord[None, :] - cells[:, 1][:, None]) % span_total
    onehot_y = ((offset_y <= DISK) | (offset_y >= span_total - DISK)).astype(jnp.float32)
    offset_z = jnp.abs(jnp.arange(count_z, dtype=jnp.int32)[None, :] - cells[:, 2][:, None])
    onehot_z = (offset_z <= DISK).astype(jnp.float32)
    cross_yz = (onehot_y[:, :, None] * onehot_z[:, None, :]).reshape(cells.shape[0], -1)
    field = jnp.dot(onehot_x.T, cross_yz, precision=highest)
    return field.reshape(NX, ycoord.shape[0], count_z)


def column_solve(columns, local_modes):
    cells_y = columns.shape[1]
    cells_z = columns.shape[2]
    ids_y = np.arange(cells_y)
    cas_y = jnp.asarray(cas_table(ids_y, cells_y).astype(np.float32))
    cos_z = jnp.asarray(cosine_np(cells_z).astype(np.float32))
    wave_y = 2.0 * np.pi * signed_np(cells_y) / cells_y
    back_p = cas_table(ids_y, cells_y) / cells_y
    back_g = wave_y[:, None] * cas_table((-ids_y) % cells_y, cells_y) / cells_y
    back_y = jnp.asarray(np.stack([back_p, back_g]).astype(np.float32))
    first = jnp.einsum("jy,ryz->rjz", cas_y, columns, precision=lax.Precision.HIGH)
    second = jnp.einsum("rjz,mz->rjm", first, cos_z, precision=lax.Precision.HIGH)
    kz_sq = (jnp.pi * jnp.arange(cells_z, dtype=jnp.int32).astype(jnp.float32) / cells_z) ** 2
    eigen = (
        wave_square(local_modes, NX)[:, None, None]
        + wave_square(jnp.arange(cells_y, dtype=jnp.int32), cells_y)[None, :, None]
        + kz_sq[None, None, :]
        + screen
    )
    p_hat = -second / eigen
    back = jnp.einsum("gjy,rjm->rgym", back_y, p_hat, precision=lax.Precision.HIGH)
    return jnp.einsum("rgym,mz->rgyz", back, cos_z, precision=lax.Precision.HIGH)


def halo(block, cols):
    secs = lax.axis_size("sec")
    up = lambda s: [(s * cols + i, s * cols + (i + 1) % cols) for i in range(cols)]
    down = lambda s: [(s * cols + (i + 1) % cols, s * cols + i) for i in range(cols)]
    first = sum([up(s) if s % 2 == 0 else down(s) for s in range(secs)], [])
    second = sum([down(s) if s % 2 == 0 else up(s) for s in range(secs)], [])
    got_first = lax.ppermute(block, ("sec", "col"), first)
    got_second = lax.ppermute(block, ("sec", "col"), second)
    even = lax.axis_index("sec") % 2 == 0
    low = jnp.where(even, got_first, got_second)
    high = jnp.where(even, got_second, got_first)
    return low, high


def local(velocity, thrust, band_counts, farm_split, turbine_cells):
    moving_bf = velocity[0]
    rows_here = moving_bf.shape[2]
    count_z = moving_bf.shape[3]
    col_index = lax.axis_index("col")
    cols = lax.axis_size("col")
    span_total = rows_here * cols
    farm_on = (lax.axis_index("sec") == 1).astype(jnp.float32)
    deriv_bf = deriv_table()
    modes_np = slot_modes()
    cas_x = jnp.asarray(cas_table(modes_np, NX).astype(np.float32))

    low, high = halo(moving_bf, cols)
    outflow = lax.ppermute(moving_bf[:, NX - FR :], "sec", [(0, 1)])

    moving = moving_bf.astype(jnp.float32)
    along_x = jnp.einsum("ij,cjyz->ciyz", deriv_bf, moving_bf, preferred_element_type=jnp.float32)
    along_y = (high.astype(jnp.float32) - low.astype(jnp.float32)) * 0.5
    along_z = zdiff(moving)
    advection = moving[0] * along_x + moving[1] * along_y + moving[2] * along_z
    weights = fringe_weights(farm_split[0]) * farm_on
    target = jnp.einsum("xj,cjyz->cxyz", weights, outflow.astype(jnp.float32), precision=highest)
    fringe = target - jnp.sum(weights, axis=1)[None, :, None, None] * moving
    ycoord = col_index * rows_here + jnp.arange(rows_here, dtype=jnp.int32)
    drag_field = turbine_field(turbine_cells, thrust, ycoord, count_z, span_total) * farm_on
    thrust_force = -0.5 * drag_field * moving[0] * jnp.abs(moving[0])
    tendency = -advection + fringe
    ustar_one = (moving[1] + time_step * tendency[1]).astype(jnp.bfloat16)
    side_low, side_high = halo(ustar_one, cols)
    ustar_one, held = lax.optimization_barrier((ustar_one, moving_bf))
    held = held.astype(jnp.float32)
    tendency = jnp.concatenate([tendency[:1] + thrust_force[None], tendency[1:]], axis=0)
    ustar = (held + time_step * tendency).astype(jnp.bfloat16)
    ustar = jnp.concatenate([ustar[:1], ustar_one[None], ustar[2:]], axis=0)
    side_low = side_low.astype(jnp.float32)
    side_high = side_high.astype(jnp.float32)
    ustar_f = ustar.astype(jnp.float32)
    divergence = jnp.einsum("ij,jyz->iyz", deriv_bf, ustar[0], preferred_element_type=jnp.float32)
    divergence = divergence + (side_high - side_low) * 0.5
    divergence = divergence + zdiff(ustar_f[2])
    source = divergence / time_step
    modes = jnp.asarray(modes_np.astype(np.int32))
    retained = kept_mask(modes, band_counts[0])
    spec = jnp.einsum("kx,xyz->kyz", cas_x, source, precision=lax.Precision.HIGH) * retained[:, None, None]
    columns = lax.all_to_all(spec, "col", split_axis=0, concat_axis=1, tiled=True)
    per_device = columns.shape[0]
    local_modes = lax.dynamic_slice_in_dim(modes, col_index * per_device, per_device)
    solved = column_solve(columns, local_modes)
    back = lax.all_to_all(solved, "col", split_axis=2, concat_axis=0, tiled=True)
    pres_modes = back[:, 0]
    grad_modes = back[:, 1]
    signed = np.where(modes_np < NX // 2, modes_np, modes_np - NX).astype(np.float32)
    mirrored = jnp.concatenate([pres_modes[:1], jnp.flip(pres_modes[1:], axis=0)], axis=0)
    dx_modes = -jnp.asarray(signed)[:, None, None] * mirrored
    stacked = jnp.stack([pres_modes, dx_modes, grad_modes], axis=0)
    fields = jnp.einsum("kx,gkyz->gxyz", cas_x, stacked, precision=lax.Precision.HIGH) / NX
    pressure = fields[0]
    grad_x = fields[1]
    grad_y = fields[2]
    grad_z = zdiff(pressure)
    newer = ustar_f - time_step * jnp.stack([grad_x, grad_y, grad_z], axis=0)
    return (newer.astype(jnp.bfloat16)[None], pressure[None])


def solution(mesh):
    return jax.shard_map(
        local,
        mesh=mesh,
        in_specs=(P("sec", None, None, "col", None), P(), P("sec", None), P(), P()),
        out_specs=(P("sec", None, None, "col", None), P("sec", None, "col", None)),
        check_vma=False,
    )
```

```python
import numpy as np
import jax
import jax.numpy as jnp
from jax import lax
from jax.sharding import PartitionSpec as P

NX = 1024
BAND = 32
NB = 10
FR = 32
DISK = 4
KX = 320
SLOTS = 2 * KX


highest = lax.Precision.HIGHEST
time_step = 0.25
screen = 0.01
fringe_rate = 2.0


def slot_modes():
    slots = np.arange(SLOTS)
    return np.where(slots < KX, slots, slots + NX - SLOTS)


def deriv_table():
    index = np.arange(NX)
    offset = (index[:, None] - index[None, :]) % NX
    angle = np.pi * offset / NX
    parity = 1.0 - 2.0 * (offset % 2)
    denom = np.where(offset == 0, 1.0, np.sin(angle))
    table = np.where(offset == 0, 0.0, 0.5 * parity * np.cos(angle) / denom)
    return jnp.asarray(table.astype(np.float32)).astype(jnp.bfloat16)


def cas_table(modes, length):
    cells = np.arange(length)
    angle = 2.0 * np.pi * ((modes[:, None] * cells[None, :]) % length) / length
    return np.cos(angle) + np.sin(angle)


def cosine_np(length):
    index = np.arange(length)
    angle = np.pi * index[:, None] * (2 * index[None, :] + 1) / (2 * length)
    scale = np.where(index == 0, np.sqrt(1.0 / length), np.sqrt(2.0 / length))
    return np.cos(angle) * scale[:, None]


def signed_np(length):
    index = np.arange(length)
    return np.where(index < length // 2, index, np.where(index > length // 2, index - length, 0))


def wave_square(mode_ids, length):
    folded = jnp.minimum(mode_ids, length - mode_ids).astype(jnp.float32)
    return (2.0 * jnp.pi * folded / length) ** 2


def kept_mask(mode_ids, counts):
    folded = jnp.minimum(mode_ids, NX - mode_ids)
    band_of = folded // BAND
    onehot = band_of[:, None] == jnp.arange(NB, dtype=jnp.int32)[None, :]
    limit_per = jnp.sum(jnp.where(onehot, counts[None, :], 0), axis=1)
    return ((folded < KX) & (folded % BAND < limit_per)).astype(jnp.float32)


def zdiff(field):
    zeros = jnp.zeros(field.shape[:-1] + (1,), jnp.float32)
    upper = jnp.concatenate([field[..., 1:], zeros], axis=-1)
    lower = jnp.concatenate([zeros, field[..., :-1]], axis=-1)
    return (upper - lower) * 0.5


def fringe_weights(split_at):
    cells = jnp.arange(NX, dtype=jnp.int32)[:, None]
    plane = jnp.arange(FR, dtype=jnp.int32)[None, :]
    rate = fringe_rate * jnp.sin(jnp.pi * (plane.astype(jnp.float32) + 0.5) / FR) ** 2
    inside = (cells == plane) | (cells == split_at + plane)
    return jnp.where(inside, rate, 0.0)


def turbine_field(cells, thrust, ycoord, count_z, span_total):
    onehot_x = (cells[:, 0][:, None] == jnp.arange(NX, dtype=jnp.int32)[None, :]).astype(
        jnp.float32
    ) * thrust[:, None]
    offset_y = (ycoord[None, :] - cells[:, 1][:, None]) % span_total
    onehot_y = ((offset_y <= DISK) | (offset_y >= span_total - DISK)).astype(jnp.float32)
    offset_z = jnp.abs(jnp.arange(count_z, dtype=jnp.int32)[None, :] - cells[:, 2][:, None])
    onehot_z = (offset_z <= DISK).astype(jnp.float32)
    cross_yz = (onehot_y[:, :, None] * onehot_z[:, None, :]).reshape(cells.shape[0], -1)
    field = jnp.dot(onehot_x.T, cross_yz, precision=highest)
    return field.reshape(NX, ycoord.shape[0], count_z)


def column_solve(columns, local_modes):
    cells_y = columns.shape[1]
    cells_z = columns.shape[2]
    ids_y = np.arange(cells_y)
    cas_y = jnp.asarray(cas_table(ids_y, cells_y).astype(np.float32))
    cos_z = jnp.asarray(cosine_np(cells_z).astype(np.float32))
    wave_y = 2.0 * np.pi * signed_np(cells_y) / cells_y
    back_p = cas_table(ids_y, cells_y) / cells_y
    back_g = wave_y[:, None] * cas_table((-ids_y) % cells_y, cells_y) / cells_y
    back_y = jnp.asarray(np.stack([back_p, back_g]).astype(np.float32))
    first = jnp.einsum("jy,ryz->rjz", cas_y, columns, precision=lax.Precision.HIGH)
    second = jnp.einsum("rjz,mz->rjm", first, cos_z, precision=lax.Precision.HIGH)
    kz_sq = (jnp.pi * jnp.arange(cells_z, dtype=jnp.int32).astype(jnp.float32) / cells_z) ** 2
    eigen = (
        wave_square(local_modes, NX)[:, None, None]
        + wave_square(jnp.arange(cells_y, dtype=jnp.int32), cells_y)[None, :, None]
        + kz_sq[None, None, :]
        + screen
    )
    p_hat = -second / eigen
    back = jnp.einsum("gjy,rjm->rgym", back_y, p_hat, precision=lax.Precision.HIGH)
    return jnp.einsum("rgym,mz->rgyz", back, cos_z, precision=lax.Precision.HIGH)


def halo(block, cols):
    secs = lax.axis_size("sec")
    up = lambda s: [(s * cols + i, s * cols + (i + 1) % cols) for i in range(cols)]
    down = lambda s: [(s * cols + (i + 1) % cols, s * cols + i) for i in range(cols)]
    first = sum([up(s) if s % 2 == 0 else down(s) for s in range(secs)], [])
    second = sum([down(s) if s % 2 == 0 else up(s) for s in range(secs)], [])
    got_first = lax.ppermute(block, ("sec", "col"), first)
    got_second = lax.ppermute(block, ("sec", "col"), second)
    even = lax.axis_index("sec") % 2 == 0
    low = jnp.where(even, got_first, got_second)
    high = jnp.where(even, got_second, got_first)
    return low, high


def local(velocity, thrust, band_counts, farm_split, turbine_cells):
    moving_bf = velocity[0]
    rows_here = moving_bf.shape[2]
    count_z = moving_bf.shape[3]
    col_index = lax.axis_index("col")
    cols = lax.axis_size("col")
    span_total = rows_here * cols
    farm_on = (lax.axis_index("sec") == 1).astype(jnp.float32)
    deriv_bf = deriv_table()
    modes_np = slot_modes()
    cas_x = jnp.asarray(cas_table(modes_np, NX).astype(np.float32))

    low, high = halo(moving_bf, cols)
    outflow = lax.ppermute(moving_bf[:, NX - FR :], "sec", [(0, 1)])

    moving = moving_bf.astype(jnp.float32)
    along_x = jnp.einsum("ij,cjyz->ciyz", deriv_bf, moving_bf, preferred_element_type=jnp.float32)
    along_z = zdiff(moving)
    weights = fringe_weights(farm_split[0]) * farm_on
    target = jnp.einsum("xj,cjyz->cxyz", weights, outflow.astype(jnp.float32), precision=highest)
    fringe = target - jnp.sum(weights, axis=1)[None, :, None, None] * moving
    ycoord = col_index * rows_here + jnp.arange(rows_here, dtype=jnp.int32)
    drag_field = turbine_field(turbine_cells, thrust, ycoord, count_z, span_total) * farm_on
    thrust_force = -0.5 * drag_field * moving[0] * jnp.abs(moving[0])
    local_part = -(moving[0] * along_x + moving[2] * along_z) + fringe
    local_part = jnp.concatenate([local_part[:1] + thrust_force[None], local_part[1:]], axis=0)
    local_part = lax.optimization_barrier(local_part)
    along_y = (high.astype(jnp.float32) - low.astype(jnp.float32)) * 0.5
    tendency = local_part - moving[1] * along_y
    ustar = (moving + time_step * tendency).astype(jnp.bfloat16)
    side_low, side_high = halo(ustar[1], cols)
    side_low = side_low.astype(jnp.float32)
    side_high = side_high.astype(jnp.float32)
    ustar_f = ustar.astype(jnp.float32)
    divergence = jnp.einsum("ij,jyz->iyz", deriv_bf, ustar[0], preferred_element_type=jnp.float32)
    divergence = divergence + (side_high - side_low) * 0.5
    divergence = divergence + zdiff(ustar_f[2])
    source = divergence / time_step
    modes = jnp.asarray(modes_np.astype(np.int32))
    retained = kept_mask(modes, band_counts[0])
    spec = jnp.einsum("kx,xyz->kyz", cas_x, source, precision=lax.Precision.HIGH) * retained[:, None, None]
    columns = lax.all_to_all(spec, "col", split_axis=0, concat_axis=1, tiled=True)
    per_device = columns.shape[0]
    local_modes = lax.dynamic_slice_in_dim(modes, col_index * per_device, per_device)
    solved = column_solve(columns, local_modes)
    back = lax.all_to_all(solved, "col", split_axis=2, concat_axis=0, tiled=True)
    pres_modes = back[:, 0]
    grad_modes = back[:, 1]
    signed = np.where(modes_np < NX // 2, modes_np, modes_np - NX).astype(np.float32)
    mirrored = jnp.concatenate([pres_modes[:1], jnp.flip(pres_modes[1:], axis=0)], axis=0)
    dx_modes = -jnp.asarray(signed)[:, None, None] * mirrored
    stacked = jnp.stack([pres_modes, dx_modes, grad_modes], axis=0)
    fields = jnp.einsum("kx,gkyz->gxyz", cas_x, stacked, precision=lax.Precision.HIGH) / NX
    pressure = fields[0]
    grad_x = fields[1]
    grad_y = fields[2]
    grad_z = zdiff(pressure)
    newer = ustar_f - time_step * jnp.stack([grad_x, grad_y, grad_z], axis=0)
    return (newer.astype(jnp.bfloat16)[None], pressure[None])


def solution(mesh):
    return jax.shard_map(
        local,
        mesh=mesh,
        in_specs=(P("sec", None, None, "col", None), P(), P("sec", None), P(), P()),
        out_specs=(P("sec", None, None, "col", None), P("sec", None, "col", None)),
        check_vma=False,
    )
```

```python
import numpy as np
import jax
import jax.numpy as jnp
from jax import lax
from jax.sharding import PartitionSpec as P

NX = 1024
BAND = 32
NB = 10
FR = 32
DISK = 4
KX = 320
SLOTS = 2 * KX


highest = lax.Precision.HIGHEST
time_step = 0.25
screen = 0.01
fringe_rate = 2.0


def slot_modes():
    slots = np.arange(SLOTS)
    return np.where(slots < KX, slots, slots + NX - SLOTS)


def deriv_table():
    index = np.arange(NX)
    offset = (index[:, None] - index[None, :]) % NX
    angle = np.pi * offset / NX
    parity = 1.0 - 2.0 * (offset % 2)
    denom = np.where(offset == 0, 1.0, np.sin(angle))
    table = np.where(offset == 0, 0.0, 0.5 * parity * np.cos(angle) / denom)
    return jnp.asarray(table.astype(np.float32)).astype(jnp.bfloat16)


def cas_table(modes, length):
    cells = np.arange(length)
    angle = 2.0 * np.pi * ((modes[:, None] * cells[None, :]) % length) / length
    return np.cos(angle) + np.sin(angle)


def cosine_np(length):
    index = np.arange(length)
    angle = np.pi * index[:, None] * (2 * index[None, :] + 1) / (2 * length)
    scale = np.where(index == 0, np.sqrt(1.0 / length), np.sqrt(2.0 / length))
    return np.cos(angle) * scale[:, None]


def signed_np(length):
    index = np.arange(length)
    return np.where(index < length // 2, index, np.where(index > length // 2, index - length, 0))


def wave_square(mode_ids, length):
    folded = jnp.minimum(mode_ids, length - mode_ids).astype(jnp.float32)
    return (2.0 * jnp.pi * folded / length) ** 2


def kept_mask(mode_ids, counts):
    folded = jnp.minimum(mode_ids, NX - mode_ids)
    band_of = folded // BAND
    onehot = band_of[:, None] == jnp.arange(NB, dtype=jnp.int32)[None, :]
    limit_per = jnp.sum(jnp.where(onehot, counts[None, :], 0), axis=1)
    return ((folded < KX) & (folded % BAND < limit_per)).astype(jnp.float32)


def zdiff(field):
    zeros = jnp.zeros(field.shape[:-1] + (1,), jnp.float32)
    upper = jnp.concatenate([field[..., 1:], zeros], axis=-1)
    lower = jnp.concatenate([zeros, field[..., :-1]], axis=-1)
    return (upper - lower) * 0.5


def fringe_weights(split_at):
    cells = jnp.arange(NX, dtype=jnp.int32)[:, None]
    plane = jnp.arange(FR, dtype=jnp.int32)[None, :]
    rate = fringe_rate * jnp.sin(jnp.pi * (plane.astype(jnp.float32) + 0.5) / FR) ** 2
    inside = (cells == plane) | (cells == split_at + plane)
    return jnp.where(inside, rate, 0.0)


def turbine_field(cells, thrust, ycoord, count_z, span_total):
    onehot_x = (cells[:, 0][:, None] == jnp.arange(NX, dtype=jnp.int32)[None, :]).astype(
        jnp.float32
    ) * thrust[:, None]
    offset_y = (ycoord[None, :] - cells[:, 1][:, None]) % span_total
    onehot_y = ((offset_y <= DISK) | (offset_y >= span_total - DISK)).astype(jnp.float32)
    offset_z = jnp.abs(jnp.arange(count_z, dtype=jnp.int32)[None, :] - cells[:, 2][:, None])
    onehot_z = (offset_z <= DISK).astype(jnp.float32)
    cross_yz = (onehot_y[:, :, None] * onehot_z[:, None, :]).reshape(cells.shape[0], -1)
    field = jnp.dot(onehot_x.T, cross_yz, precision=highest)
    return field.reshape(NX, ycoord.shape[0], count_z)


def column_solve(columns, local_modes):
    cells_y = columns.shape[1]
    cells_z = columns.shape[2]
    ids_y = np.arange(cells_y)
    cas_y = jnp.asarray(cas_table(ids_y, cells_y).astype(np.float32))
    cos_z = jnp.asarray(cosine_np(cells_z).astype(np.float32))
    wave_y = 2.0 * np.pi * signed_np(cells_y) / cells_y
    back_p = cas_table(ids_y, cells_y) / cells_y
    back_g = wave_y[:, None] * cas_table((-ids_y) % cells_y, cells_y) / cells_y
    back_y = jnp.asarray(np.stack([back_p, back_g]).astype(np.float32))
    first = jnp.einsum("jy,ryz->rjz", cas_y, columns, precision=lax.Precision.HIGH)
    second = jnp.einsum("rjz,mz->rjm", first, cos_z, precision=lax.Precision.HIGH)
    kz_sq = (jnp.pi * jnp.arange(cells_z, dtype=jnp.int32).astype(jnp.float32) / cells_z) ** 2
    eigen = (
        wave_square(local_modes, NX)[:, None, None]
        + wave_square(jnp.arange(cells_y, dtype=jnp.int32), cells_y)[None, :, None]
        + kz_sq[None, None, :]
        + screen
    )
    p_hat = -second / eigen
    back = jnp.einsum("gjy,rjm->rgym", back_y, p_hat, precision=lax.Precision.HIGH)
    return jnp.einsum("rgym,mz->rgyz", back, cos_z, precision=lax.Precision.HIGH)


def halo(block, cols):
    secs = lax.axis_size("sec")
    up = lambda s: [(s * cols + i, s * cols + (i + 1) % cols) for i in range(cols)]
    down = lambda s: [(s * cols + (i + 1) % cols, s * cols + i) for i in range(cols)]
    first = sum([up(s) if s % 2 == 0 else down(s) for s in range(secs)], [])
    second = sum([down(s) if s % 2 == 0 else up(s) for s in range(secs)], [])
    got_first = lax.ppermute(block, ("sec", "col"), first)
    got_second = lax.ppermute(block, ("sec", "col"), second)
    even = lax.axis_index("sec") % 2 == 0
    low = jnp.where(even, got_first, got_second)
    high = jnp.where(even, got_second, got_first)
    return low, high


def local(velocity, thrust, band_counts, farm_split, turbine_cells):
    moving_bf = velocity[0]
    rows_here = moving_bf.shape[2]
    count_z = moving_bf.shape[3]
    col_index = lax.axis_index("col")
    cols = lax.axis_size("col")
    span_total = rows_here * cols
    farm_on = (lax.axis_index("sec") == 1).astype(jnp.float32)
    deriv_bf = deriv_table()
    modes_np = slot_modes()
    cas_x = jnp.asarray(cas_table(modes_np, NX).astype(np.float32))

    low, high = halo(moving_bf, cols)
    outflow = lax.ppermute(moving_bf[:, NX - FR :], "sec", [(0, 1)])

    moving = moving_bf.astype(jnp.float32)
    along_x = jnp.einsum("ij,cjyz->ciyz", deriv_bf, moving_bf, preferred_element_type=jnp.float32)
    along_z = zdiff(moving)
    weights = fringe_weights(farm_split[0]) * farm_on
    target = jnp.einsum("xj,cjyz->cxyz", weights, outflow.astype(jnp.float32), precision=highest)
    fringe = target - jnp.sum(weights, axis=1)[None, :, None, None] * moving
    ycoord = col_index * rows_here + jnp.arange(rows_here, dtype=jnp.int32)
    drag_field = turbine_field(turbine_cells, thrust, ycoord, count_z, span_total) * farm_on
    thrust_force = -0.5 * drag_field * moving[0] * jnp.abs(moving[0])
    local_part = -(moving[0] * along_x + moving[2] * along_z) + fringe
    local_part = jnp.concatenate([local_part[:1] + thrust_force[None], local_part[1:]], axis=0)
    local_part = lax.optimization_barrier(local_part)
    along_y = (high.astype(jnp.float32) - low.astype(jnp.float32)) * 0.5
    tendency = local_part - moving[1] * along_y
    ustar = (moving + time_step * tendency).astype(jnp.bfloat16)
    side_low, side_high = halo(ustar[1], cols)
    ustar_f = ustar.astype(jnp.float32)
    divergence = jnp.einsum("ij,jyz->iyz", deriv_bf, ustar[0], preferred_element_type=jnp.float32)
    divergence = lax.optimization_barrier(divergence + zdiff(ustar_f[2]))
    side_low = side_low.astype(jnp.float32)
    side_high = side_high.astype(jnp.float32)
    divergence = divergence + (side_high - side_low) * 0.5
    source = divergence / time_step
    modes = jnp.asarray(modes_np.astype(np.int32))
    retained = kept_mask(modes, band_counts[0])
    spec = jnp.einsum("kx,xyz->kyz", cas_x, source, precision=lax.Precision.HIGH) * retained[:, None, None]
    columns = lax.all_to_all(spec, "col", split_axis=0, concat_axis=1, tiled=True)
    per_device = columns.shape[0]
    local_modes = lax.dynamic_slice_in_dim(modes, col_index * per_device, per_device)
    solved = column_solve(columns, local_modes)
    back = lax.all_to_all(solved, "col", split_axis=2, concat_axis=0, tiled=True)
    pres_modes = back[:, 0]
    grad_modes = back[:, 1]
    signed = np.where(modes_np < NX // 2, modes_np, modes_np - NX).astype(np.float32)
    mirrored = jnp.concatenate([pres_modes[:1], jnp.flip(pres_modes[1:], axis=0)], axis=0)
    dx_modes = -jnp.asarray(signed)[:, None, None] * mirrored
    stacked = jnp.stack([pres_modes, dx_modes, grad_modes], axis=0)
    fields = jnp.einsum("kx,gkyz->gxyz", cas_x, stacked, precision=lax.Precision.HIGH) / NX
    pressure = fields[0]
    grad_x = fields[1]
    grad_y = fields[2]
    grad_z = zdiff(pressure)
    newer = ustar_f - time_step * jnp.stack([grad_x, grad_y, grad_z], axis=0)
    return (newer.astype(jnp.bfloat16)[None], pressure[None])


def solution(mesh):
    return jax.shard_map(
        local,
        mesh=mesh,
        in_specs=(P("sec", None, None, "col", None), P(), P("sec", None), P(), P()),
        out_specs=(P("sec", None, None, "col", None), P("sec", None, "col", None)),
        check_vma=False,
    )
```

```python
import numpy as np
import jax
import jax.numpy as jnp
from jax import lax
from jax.sharding import PartitionSpec as P

NX = 1024
BAND = 32
NB = 10
FR = 32
DISK = 4
KX = 320
SLOTS = 2 * KX


highest = lax.Precision.HIGHEST
time_step = 0.25
screen = 0.01
fringe_rate = 2.0


def slot_modes():
    slots = np.arange(SLOTS)
    return np.where(slots < KX, slots, slots + NX - SLOTS)


def deriv_table():
    index = np.arange(NX)
    offset = (index[:, None] - index[None, :]) % NX
    angle = np.pi * offset / NX
    parity = 1.0 - 2.0 * (offset % 2)
    denom = np.where(offset == 0, 1.0, np.sin(angle))
    table = np.where(offset == 0, 0.0, 0.5 * parity * np.cos(angle) / denom)
    return jnp.asarray(table.astype(np.float32)).astype(jnp.bfloat16)


def cas_table(modes, length):
    cells = np.arange(length)
    angle = 2.0 * np.pi * ((modes[:, None] * cells[None, :]) % length) / length
    return np.cos(angle) + np.sin(angle)


def cosine_np(length):
    index = np.arange(length)
    angle = np.pi * index[:, None] * (2 * index[None, :] + 1) / (2 * length)
    scale = np.where(index == 0, np.sqrt(1.0 / length), np.sqrt(2.0 / length))
    return np.cos(angle) * scale[:, None]


def signed_np(length):
    index = np.arange(length)
    return np.where(index < length // 2, index, np.where(index > length // 2, index - length, 0))


def wave_square(mode_ids, length):
    folded = jnp.minimum(mode_ids, length - mode_ids).astype(jnp.float32)
    return (2.0 * jnp.pi * folded / length) ** 2


def kept_mask(mode_ids, counts):
    folded = jnp.minimum(mode_ids, NX - mode_ids)
    band_of = folded // BAND
    onehot = band_of[:, None] == jnp.arange(NB, dtype=jnp.int32)[None, :]
    limit_per = jnp.sum(jnp.where(onehot, counts[None, :], 0), axis=1)
    return ((folded < KX) & (folded % BAND < limit_per)).astype(jnp.float32)


def zdiff(field):
    zeros = jnp.zeros(field.shape[:-1] + (1,), jnp.float32)
    upper = jnp.concatenate([field[..., 1:], zeros], axis=-1)
    lower = jnp.concatenate([zeros, field[..., :-1]], axis=-1)
    return (upper - lower) * 0.5


def fringe_weights(split_at):
    cells = jnp.arange(NX, dtype=jnp.int32)[:, None]
    plane = jnp.arange(FR, dtype=jnp.int32)[None, :]
    rate = fringe_rate * jnp.sin(jnp.pi * (plane.astype(jnp.float32) + 0.5) / FR) ** 2
    inside = (cells == plane) | (cells == split_at + plane)
    return jnp.where(inside, rate, 0.0)


def turbine_field(cells, thrust, ycoord, count_z, span_total):
    onehot_x = (cells[:, 0][:, None] == jnp.arange(NX, dtype=jnp.int32)[None, :]).astype(
        jnp.float32
    ) * thrust[:, None]
    offset_y = (ycoord[None, :] - cells[:, 1][:, None]) % span_total
    onehot_y = ((offset_y <= DISK) | (offset_y >= span_total - DISK)).astype(jnp.float32)
    offset_z = jnp.abs(jnp.arange(count_z, dtype=jnp.int32)[None, :] - cells[:, 2][:, None])
    onehot_z = (offset_z <= DISK).astype(jnp.float32)
    cross_yz = (onehot_y[:, :, None] * onehot_z[:, None, :]).reshape(cells.shape[0], -1)
    field = jnp.dot(onehot_x.T, cross_yz, precision=highest)
    return field.reshape(NX, ycoord.shape[0], count_z)


def column_solve(columns, local_modes):
    cells_y = columns.shape[1]
    cells_z = columns.shape[2]
    ids_y = np.arange(cells_y)
    cas_y = jnp.asarray(cas_table(ids_y, cells_y).astype(np.float32))
    cos_z = jnp.asarray(cosine_np(cells_z).astype(np.float32))
    wave_y = 2.0 * np.pi * signed_np(cells_y) / cells_y
    back_p = cas_table(ids_y, cells_y) / cells_y
    back_g = wave_y[:, None] * cas_table((-ids_y) % cells_y, cells_y) / cells_y
    back_y = jnp.asarray(np.stack([back_p, back_g]).astype(np.float32))
    first = jnp.einsum("jy,ryz->rjz", cas_y, columns, precision=lax.Precision.HIGH)
    second = jnp.einsum("rjz,mz->rjm", first, cos_z, precision=lax.Precision.HIGH)
    kz_sq = (jnp.pi * jnp.arange(cells_z, dtype=jnp.int32).astype(jnp.float32) / cells_z) ** 2
    eigen = (
        wave_square(local_modes, NX)[:, None, None]
        + wave_square(jnp.arange(cells_y, dtype=jnp.int32), cells_y)[None, :, None]
        + kz_sq[None, None, :]
        + screen
    )
    p_hat = -second / eigen
    back = jnp.einsum("gjy,rjm->rgym", back_y, p_hat, precision=lax.Precision.HIGH)
    return jnp.einsum("rgym,mz->rgyz", back, cos_z, precision=lax.Precision.HIGH)


def halo(block, cols):
    secs = lax.axis_size("sec")
    up = lambda s: [(s * cols + i, s * cols + (i + 1) % cols) for i in range(cols)]
    down = lambda s: [(s * cols + (i + 1) % cols, s * cols + i) for i in range(cols)]
    first = sum([up(s) if s % 2 == 0 else down(s) for s in range(secs)], [])
    second = sum([down(s) if s % 2 == 0 else up(s) for s in range(secs)], [])
    got_first = lax.ppermute(block, ("sec", "col"), first)
    got_second = lax.ppermute(block, ("sec", "col"), second)
    even = lax.axis_index("sec") % 2 == 0
    low = jnp.where(even, got_first, got_second)
    high = jnp.where(even, got_second, got_first)
    return low, high


def local(velocity, thrust, band_counts, farm_split, turbine_cells):
    moving_bf = velocity[0]
    rows_here = moving_bf.shape[2]
    count_z = moving_bf.shape[3]
    col_index = lax.axis_index("col")
    cols = lax.axis_size("col")
    span_total = rows_here * cols
    farm_on = (lax.axis_index("sec") == 1).astype(jnp.float32)
    deriv_bf = deriv_table()
    modes_np = slot_modes()
    cas_x = jnp.asarray(cas_table(modes_np, NX).astype(np.float32))

    low, high = halo(moving_bf, cols)
    outflow = lax.ppermute(moving_bf[:, NX - FR :], "sec", [(0, 1)])

    moving = moving_bf.astype(jnp.float32)
    along_x = jnp.einsum("ij,cjyz->ciyz", deriv_bf, moving_bf, preferred_element_type=jnp.float32)
    along_z = zdiff(moving)
    weights = fringe_weights(farm_split[0]) * farm_on
    target = jnp.einsum("xj,cjyz->cxyz", weights, outflow.astype(jnp.float32), precision=highest)
    fringe = target - jnp.sum(weights, axis=1)[None, :, None, None] * moving
    ycoord = col_index * rows_here + jnp.arange(rows_here, dtype=jnp.int32)
    drag_field = turbine_field(turbine_cells, thrust, ycoord, count_z, span_total) * farm_on
    thrust_force = -0.5 * drag_field * moving[0] * jnp.abs(moving[0])
    local_part = -(moving[0] * along_x + moving[2] * along_z) + fringe
    local_part = jnp.concatenate([local_part[:1] + thrust_force[None], local_part[1:]], axis=0)
    local_part = lax.optimization_barrier(local_part)
    def predict(part, below, above, comps):
        spanwise = (above[comps].astype(jnp.float32) - below[comps].astype(jnp.float32)) * 0.5
        tend = part[comps] - moving[1] * spanwise
        return (moving[comps] + time_step * tend).astype(jnp.bfloat16)

    ustar_one = predict(local_part, low, high, slice(1, 2))
    side_low, side_high = halo(ustar_one[0], cols)
    ustar_one, local_part, low, high = lax.optimization_barrier((ustar_one, local_part, low, high))
    ustar = jnp.concatenate(
        [predict(local_part, low, high, slice(0, 1)), ustar_one, predict(local_part, low, high, slice(2, 3))],
        axis=0,
    )
    ustar_f = ustar.astype(jnp.float32)
    divergence = jnp.einsum("ij,jyz->iyz", deriv_bf, ustar[0], preferred_element_type=jnp.float32)
    divergence = lax.optimization_barrier(divergence + zdiff(ustar_f[2]))
    side_low = side_low.astype(jnp.float32)
    side_high = side_high.astype(jnp.float32)
    divergence = divergence + (side_high - side_low) * 0.5
    source = divergence / time_step
    modes = jnp.asarray(modes_np.astype(np.int32))
    retained = kept_mask(modes, band_counts[0])
    spec = jnp.einsum("kx,xyz->kyz", cas_x, source, precision=lax.Precision.HIGH) * retained[:, None, None]
    columns = lax.all_to_all(spec, "col", split_axis=0, concat_axis=1, tiled=True)
    per_device = columns.shape[0]
    local_modes = lax.dynamic_slice_in_dim(modes, col_index * per_device, per_device)
    solved = column_solve(columns, local_modes)
    back = lax.all_to_all(solved, "col", split_axis=2, concat_axis=0, tiled=True)
    pres_modes = back[:, 0]
    grad_modes = back[:, 1]
    signed = np.where(modes_np < NX // 2, modes_np, modes_np - NX).astype(np.float32)
    mirrored = jnp.concatenate([pres_modes[:1], jnp.flip(pres_modes[1:], axis=0)], axis=0)
    dx_modes = -jnp.asarray(signed)[:, None, None] * mirrored
    stacked = jnp.stack([pres_modes, dx_modes, grad_modes], axis=0)
    fields = jnp.einsum("kx,gkyz->gxyz", cas_x, stacked, precision=lax.Precision.HIGH) / NX
    pressure = fields[0]
    grad_x = fields[1]
    grad_y = fields[2]
    grad_z = zdiff(pressure)
    newer = ustar_f - time_step * jnp.stack([grad_x, grad_y, grad_z], axis=0)
    return (newer.astype(jnp.bfloat16)[None], pressure[None])


def solution(mesh):
    return jax.shard_map(
        local,
        mesh=mesh,
        in_specs=(P("sec", None, None, "col", None), P(), P("sec", None), P(), P()),
        out_specs=(P("sec", None, None, "col", None), P("sec", None, "col", None)),
        check_vma=False,
    )
```

```python
import numpy as np
import jax
import jax.numpy as jnp
from jax import lax
from jax.sharding import PartitionSpec as P

NX = 1024
BAND = 32
NB = 10
FR = 32
DISK = 4
KX = 320
SLOTS = 2 * KX


highest = lax.Precision.HIGHEST
time_step = 0.25
screen = 0.01
fringe_rate = 2.0


def slot_modes():
    slots = np.arange(SLOTS)
    return np.where(slots < KX, slots, slots + NX - SLOTS)


def deriv_table():
    index = np.arange(NX)
    offset = (index[:, None] - index[None, :]) % NX
    angle = np.pi * offset / NX
    parity = 1.0 - 2.0 * (offset % 2)
    denom = np.where(offset == 0, 1.0, np.sin(angle))
    table = np.where(offset == 0, 0.0, 0.5 * parity * np.cos(angle) / denom)
    return jnp.asarray(table.astype(np.float32)).astype(jnp.bfloat16)


def cas_table(modes, length):
    cells = np.arange(length)
    angle = 2.0 * np.pi * ((modes[:, None] * cells[None, :]) % length) / length
    return np.cos(angle) + np.sin(angle)


def cosine_np(length):
    index = np.arange(length)
    angle = np.pi * index[:, None] * (2 * index[None, :] + 1) / (2 * length)
    scale = np.where(index == 0, np.sqrt(1.0 / length), np.sqrt(2.0 / length))
    return np.cos(angle) * scale[:, None]


def signed_np(length):
    index = np.arange(length)
    return np.where(index < length // 2, index, np.where(index > length // 2, index - length, 0))


def wave_square(mode_ids, length):
    folded = jnp.minimum(mode_ids, length - mode_ids).astype(jnp.float32)
    return (2.0 * jnp.pi * folded / length) ** 2


def kept_mask(mode_ids, counts):
    folded = jnp.minimum(mode_ids, NX - mode_ids)
    band_of = folded // BAND
    onehot = band_of[:, None] == jnp.arange(NB, dtype=jnp.int32)[None, :]
    limit_per = jnp.sum(jnp.where(onehot, counts[None, :], 0), axis=1)
    return ((folded < KX) & (folded % BAND < limit_per)).astype(jnp.float32)


def zdiff(field):
    zeros = jnp.zeros(field.shape[:-1] + (1,), jnp.float32)
    upper = jnp.concatenate([field[..., 1:], zeros], axis=-1)
    lower = jnp.concatenate([zeros, field[..., :-1]], axis=-1)
    return (upper - lower) * 0.5


def fringe_weights(split_at):
    cells = jnp.arange(NX, dtype=jnp.int32)[:, None]
    plane = jnp.arange(FR, dtype=jnp.int32)[None, :]
    rate = fringe_rate * jnp.sin(jnp.pi * (plane.astype(jnp.float32) + 0.5) / FR) ** 2
    inside = (cells == plane) | (cells == split_at + plane)
    return jnp.where(inside, rate, 0.0)


def turbine_field(cells, thrust, ycoord, count_z, span_total):
    onehot_x = (cells[:, 0][:, None] == jnp.arange(NX, dtype=jnp.int32)[None, :]).astype(
        jnp.float32
    ) * thrust[:, None]
    offset_y = (ycoord[None, :] - cells[:, 1][:, None]) % span_total
    onehot_y = ((offset_y <= DISK) | (offset_y >= span_total - DISK)).astype(jnp.float32)
    offset_z = jnp.abs(jnp.arange(count_z, dtype=jnp.int32)[None, :] - cells[:, 2][:, None])
    onehot_z = (offset_z <= DISK).astype(jnp.float32)
    cross_yz = (onehot_y[:, :, None] * onehot_z[:, None, :]).reshape(cells.shape[0], -1)
    field = jnp.dot(onehot_x.T, cross_yz, precision=highest)
    return field.reshape(NX, ycoord.shape[0], count_z)


def column_solve(columns, local_modes):
    cells_y = columns.shape[1]
    cells_z = columns.shape[2]
    ids_y = np.arange(cells_y)
    cas_y = jnp.asarray(cas_table(ids_y, cells_y).astype(np.float32))
    cos_z = jnp.asarray(cosine_np(cells_z).astype(np.float32))
    wave_y = 2.0 * np.pi * signed_np(cells_y) / cells_y
    back_p = cas_table(ids_y, cells_y) / cells_y
    back_g = wave_y[:, None] * cas_table((-ids_y) % cells_y, cells_y) / cells_y
    back_y = jnp.asarray(np.stack([back_p, back_g]).astype(np.float32))
    first = jnp.einsum("jy,ryz->rjz", cas_y, columns, precision=lax.Precision.HIGH)
    second = jnp.einsum("rjz,mz->rjm", first, cos_z, precision=lax.Precision.HIGH)
    kz_sq = (jnp.pi * jnp.arange(cells_z, dtype=jnp.int32).astype(jnp.float32) / cells_z) ** 2
    eigen = (
        wave_square(local_modes, NX)[:, None, None]
        + wave_square(jnp.arange(cells_y, dtype=jnp.int32), cells_y)[None, :, None]
        + kz_sq[None, None, :]
        + screen
    )
    p_hat = -second / eigen
    back = jnp.einsum("gjy,rjm->rgym", back_y, p_hat, precision=lax.Precision.HIGH)
    return jnp.einsum("rgym,mz->rgyz", back, cos_z, precision=lax.Precision.HIGH)


def halo(block, cols):
    secs = lax.axis_size("sec")
    up = lambda s: [(s * cols + i, s * cols + (i + 1) % cols) for i in range(cols)]
    down = lambda s: [(s * cols + (i + 1) % cols, s * cols + i) for i in range(cols)]
    first = sum([up(s) if s % 2 == 0 else down(s) for s in range(secs)], [])
    second = sum([down(s) if s % 2 == 0 else up(s) for s in range(secs)], [])
    got_first = lax.ppermute(block, ("sec", "col"), first)
    got_second = lax.ppermute(block, ("sec", "col"), second)
    even = lax.axis_index("sec") % 2 == 0
    low = jnp.where(even, got_first, got_second)
    high = jnp.where(even, got_second, got_first)
    return low, high


def local(velocity, thrust, band_counts, farm_split, turbine_cells):
    moving_bf = velocity[0]
    rows_here = moving_bf.shape[2]
    count_z = moving_bf.shape[3]
    col_index = lax.axis_index("col")
    cols = lax.axis_size("col")
    span_total = rows_here * cols
    farm_on = (lax.axis_index("sec") == 1).astype(jnp.float32)
    deriv_bf = deriv_table()
    modes_np = slot_modes()
    cas_x = jnp.asarray(cas_table(modes_np, NX).astype(np.float32))

    low, high = halo(moving_bf, cols)
    outflow = lax.ppermute(moving_bf[:, NX - FR :], "sec", [(0, 1)])

    moving = moving_bf.astype(jnp.float32)
    along_x = jnp.einsum("ij,cjyz->ciyz", deriv_bf, moving_bf, preferred_element_type=jnp.float32)
    along_z = zdiff(moving)
    weights = fringe_weights(farm_split[0]) * farm_on
    target = jnp.einsum("xj,cjyz->cxyz", weights, outflow.astype(jnp.float32), precision=highest)
    fringe = target - jnp.sum(weights, axis=1)[None, :, None, None] * moving
    ycoord = col_index * rows_here + jnp.arange(rows_here, dtype=jnp.int32)
    drag_field = turbine_field(turbine_cells, thrust, ycoord, count_z, span_total) * farm_on
    thrust_force = -0.5 * drag_field * moving[0] * jnp.abs(moving[0])
    local_part = -(moving[0] * along_x + moving[2] * along_z) + fringe
    local_part = jnp.concatenate([local_part[:1] + thrust_force[None], local_part[1:]], axis=0)
    local_part = lax.optimization_barrier(local_part)
    along_y = (high.astype(jnp.float32) - low.astype(jnp.float32)) * 0.5
    tendency = local_part - moving[1] * along_y
    ustar = (moving + time_step * tendency).astype(jnp.bfloat16)
    side_low, side_high = halo(ustar[1], cols)
    ustar_f = ustar.astype(jnp.float32)
    divergence = jnp.einsum("ij,jyz->iyz", deriv_bf, ustar[0], preferred_element_type=jnp.float32)
    divergence = lax.optimization_barrier(divergence + zdiff(ustar_f[2]))
    side_low = side_low.astype(jnp.float32)
    side_high = side_high.astype(jnp.float32)
    divergence = divergence + (side_high - side_low) * 0.5
    source = divergence / time_step
    modes = jnp.asarray(modes_np.astype(np.int32))
    retained = kept_mask(modes, band_counts[0])
    spec = jnp.einsum("kx,xyz->kyz", cas_x, source, precision=lax.Precision.HIGH) * retained[:, None, None]
    columns = lax.all_to_all(spec, "col", split_axis=0, concat_axis=1, tiled=True)
    per_device = columns.shape[0]
    local_modes = lax.dynamic_slice_in_dim(modes, col_index * per_device, per_device)
    solved = column_solve(columns, local_modes)
    back = lax.all_to_all(solved, "col", split_axis=2, concat_axis=0, tiled=True)
    pres_modes = back[:, 0]
    grad_modes = back[:, 1]
    signed = np.where(modes_np < NX // 2, modes_np, modes_np - NX).astype(np.float32)
    mirrored = jnp.concatenate([pres_modes[:1], jnp.flip(pres_modes[1:], axis=0)], axis=0)
    dx_modes = -jnp.asarray(signed)[:, None, None] * mirrored
    pressure = jnp.einsum("kx,kyz->xyz", cas_x, pres_modes, precision=lax.Precision.HIGH) / NX
    stacked = jnp.stack([dx_modes, grad_modes], axis=0)
    grads = jnp.einsum("kx,gkyz->gxyz", cas_x, stacked, precision=lax.Precision.HIGH) / NX
    grad_x = grads[0]
    grad_y = grads[1]
    grad_z = zdiff(pressure)
    newer = ustar_f - time_step * jnp.stack([grad_x, grad_y, grad_z], axis=0)
    return (newer.astype(jnp.bfloat16)[None], pressure[None])


def solution(mesh):
    return jax.shard_map(
        local,
        mesh=mesh,
        in_specs=(P("sec", None, None, "col", None), P(), P("sec", None), P(), P()),
        out_specs=(P("sec", None, None, "col", None), P("sec", None, "col", None)),
        check_vma=False,
    )
```

```python
import numpy as np
import jax
import jax.numpy as jnp
from jax import lax
from jax.sharding import PartitionSpec as P

NX = 1024
BAND = 32
NB = 10
FR = 32
DISK = 4
KX = 320
SLOTS = 2 * KX


highest = lax.Precision.HIGHEST
time_step = 0.25
screen = 0.01
fringe_rate = 2.0


def slot_modes():
    slots = np.arange(SLOTS)
    return np.where(slots < KX, slots, slots + NX - SLOTS)


def deriv_table():
    index = np.arange(NX)
    offset = (index[:, None] - index[None, :]) % NX
    angle = np.pi * offset / NX
    parity = 1.0 - 2.0 * (offset % 2)
    denom = np.where(offset == 0, 1.0, np.sin(angle))
    table = np.where(offset == 0, 0.0, 0.5 * parity * np.cos(angle) / denom)
    return jnp.asarray(table.astype(np.float32)).astype(jnp.bfloat16)


def cas_table(modes, length):
    cells = np.arange(length)
    angle = 2.0 * np.pi * ((modes[:, None] * cells[None, :]) % length) / length
    return np.cos(angle) + np.sin(angle)


def cosine_np(length):
    index = np.arange(length)
    angle = np.pi * index[:, None] * (2 * index[None, :] + 1) / (2 * length)
    scale = np.where(index == 0, np.sqrt(1.0 / length), np.sqrt(2.0 / length))
    return np.cos(angle) * scale[:, None]


def signed_np(length):
    index = np.arange(length)
    return np.where(index < length // 2, index, np.where(index > length // 2, index - length, 0))


def wave_square(mode_ids, length):
    folded = jnp.minimum(mode_ids, length - mode_ids).astype(jnp.float32)
    return (2.0 * jnp.pi * folded / length) ** 2


def kept_mask(mode_ids, counts):
    folded = jnp.minimum(mode_ids, NX - mode_ids)
    band_of = folded // BAND
    onehot = band_of[:, None] == jnp.arange(NB, dtype=jnp.int32)[None, :]
    limit_per = jnp.sum(jnp.where(onehot, counts[None, :], 0), axis=1)
    return ((folded < KX) & (folded % BAND < limit_per)).astype(jnp.float32)


def zdiff(field):
    zeros = jnp.zeros(field.shape[:-1] + (1,), jnp.float32)
    upper = jnp.concatenate([field[..., 1:], zeros], axis=-1)
    lower = jnp.concatenate([zeros, field[..., :-1]], axis=-1)
    return (upper - lower) * 0.5


def fringe_weights(split_at):
    cells = jnp.arange(NX, dtype=jnp.int32)[:, None]
    plane = jnp.arange(FR, dtype=jnp.int32)[None, :]
    rate = fringe_rate * jnp.sin(jnp.pi * (plane.astype(jnp.float32) + 0.5) / FR) ** 2
    inside = (cells == plane) | (cells == split_at + plane)
    return jnp.where(inside, rate, 0.0)


def turbine_field(cells, thrust, ycoord, count_z, span_total):
    onehot_x = (cells[:, 0][:, None] == jnp.arange(NX, dtype=jnp.int32)[None, :]).astype(
        jnp.float32
    ) * thrust[:, None]
    offset_y = (ycoord[None, :] - cells[:, 1][:, None]) % span_total
    onehot_y = ((offset_y <= DISK) | (offset_y >= span_total - DISK)).astype(jnp.float32)
    offset_z = jnp.abs(jnp.arange(count_z, dtype=jnp.int32)[None, :] - cells[:, 2][:, None])
    onehot_z = (offset_z <= DISK).astype(jnp.float32)
    cross_yz = (onehot_y[:, :, None] * onehot_z[:, None, :]).reshape(cells.shape[0], -1)
    field = jnp.dot(onehot_x.T, cross_yz, precision=lax.Precision.HIGH)
    return field.reshape(NX, ycoord.shape[0], count_z)


def column_solve(columns, local_modes):
    cells_y = columns.shape[1]
    cells_z = columns.shape[2]
    ids_y = np.arange(cells_y)
    cas_y = jnp.asarray(cas_table(ids_y, cells_y).astype(np.float32))
    cos_z = jnp.asarray(cosine_np(cells_z).astype(np.float32))
    wave_y = 2.0 * np.pi * signed_np(cells_y) / cells_y
    back_p = cas_table(ids_y, cells_y) / cells_y
    back_g = wave_y[:, None] * cas_table((-ids_y) % cells_y, cells_y) / cells_y
    back_y = jnp.asarray(np.stack([back_p, back_g]).astype(np.float32))
    first = jnp.einsum("jy,ryz->rjz", cas_y, columns, precision=lax.Precision.HIGH)
    second = jnp.einsum("rjz,mz->rjm", first, cos_z, precision=lax.Precision.HIGH)
    kz_sq = (jnp.pi * jnp.arange(cells_z, dtype=jnp.int32).astype(jnp.float32) / cells_z) ** 2
    eigen = (
        wave_square(local_modes, NX)[:, None, None]
        + wave_square(jnp.arange(cells_y, dtype=jnp.int32), cells_y)[None, :, None]
        + kz_sq[None, None, :]
        + screen
    )
    p_hat = -second / eigen
    back = jnp.einsum("gjy,rjm->rgym", back_y, p_hat, precision=lax.Precision.HIGH)
    return jnp.einsum("rgym,mz->rgyz", back, cos_z, precision=lax.Precision.HIGH)


def halo(block, cols):
    secs = lax.axis_size("sec")
    up = lambda s: [(s * cols + i, s * cols + (i + 1) % cols) for i in range(cols)]
    down = lambda s: [(s * cols + (i + 1) % cols, s * cols + i) for i in range(cols)]
    first = sum([up(s) if s % 2 == 0 else down(s) for s in range(secs)], [])
    second = sum([down(s) if s % 2 == 0 else up(s) for s in range(secs)], [])
    got_first = lax.ppermute(block, ("sec", "col"), first)
    got_second = lax.ppermute(block, ("sec", "col"), second)
    even = lax.axis_index("sec") % 2 == 0
    low = jnp.where(even, got_first, got_second)
    high = jnp.where(even, got_second, got_first)
    return low, high


def local(velocity, thrust, band_counts, farm_split, turbine_cells):
    moving_bf = velocity[0]
    rows_here = moving_bf.shape[2]
    count_z = moving_bf.shape[3]
    col_index = lax.axis_index("col")
    cols = lax.axis_size("col")
    span_total = rows_here * cols
    farm_on = (lax.axis_index("sec") == 1).astype(jnp.float32)
    deriv_bf = deriv_table()
    modes_np = slot_modes()
    cas_x = jnp.asarray(cas_table(modes_np, NX).astype(np.float32))

    low, high = halo(moving_bf, cols)
    outflow = lax.ppermute(moving_bf[:, NX - FR :], "sec", [(0, 1)])

    moving = moving_bf.astype(jnp.float32)
    along_x = jnp.einsum("ij,cjyz->ciyz", deriv_bf, moving_bf, preferred_element_type=jnp.float32)
    along_z = zdiff(moving)
    weights = fringe_weights(farm_split[0]) * farm_on
    target = jnp.einsum("xj,cjyz->cxyz", weights, outflow.astype(jnp.float32), precision=lax.Precision.HIGH)
    fringe = target - jnp.sum(weights, axis=1)[None, :, None, None] * moving
    ycoord = col_index * rows_here + jnp.arange(rows_here, dtype=jnp.int32)
    drag_field = turbine_field(turbine_cells, thrust, ycoord, count_z, span_total) * farm_on
    thrust_force = -0.5 * drag_field * moving[0] * jnp.abs(moving[0])
    local_part = -(moving[0] * along_x + moving[2] * along_z) + fringe
    local_part = jnp.concatenate([local_part[:1] + thrust_force[None], local_part[1:]], axis=0)
    local_part = lax.optimization_barrier(local_part)
    along_y = (high.astype(jnp.float32) - low.astype(jnp.float32)) * 0.5
    tendency = local_part - moving[1] * along_y
    ustar = (moving + time_step * tendency).astype(jnp.bfloat16)
    side_low, side_high = halo(ustar[1], cols)
    ustar_f = ustar.astype(jnp.float32)
    divergence = jnp.einsum("ij,jyz->iyz", deriv_bf, ustar[0], preferred_element_type=jnp.float32)
    divergence = lax.optimization_barrier(divergence + zdiff(ustar_f[2]))
    side_low = side_low.astype(jnp.float32)
    side_high = side_high.astype(jnp.float32)
    divergence = divergence + (side_high - side_low) * 0.5
    source = divergence / time_step
    modes = jnp.asarray(modes_np.astype(np.int32))
    retained = kept_mask(modes, band_counts[0])
    spec = jnp.einsum("kx,xyz->kyz", cas_x, source, precision=lax.Precision.HIGH) * retained[:, None, None]
    columns = lax.all_to_all(spec, "col", split_axis=0, concat_axis=1, tiled=True)
    per_device = columns.shape[0]
    local_modes = lax.dynamic_slice_in_dim(modes, col_index * per_device, per_device)
    solved = column_solve(columns, local_modes)
    back = lax.all_to_all(solved, "col", split_axis=2, concat_axis=0, tiled=True)
    pres_modes = back[:, 0]
    grad_modes = back[:, 1]
    signed = np.where(modes_np < NX // 2, modes_np, modes_np - NX).astype(np.float32)
    mirrored = jnp.concatenate([pres_modes[:1], jnp.flip(pres_modes[1:], axis=0)], axis=0)
    dx_modes = -jnp.asarray(signed)[:, None, None] * mirrored
    stacked = jnp.stack([pres_modes, dx_modes, grad_modes], axis=0)
    fields = jnp.einsum("kx,gkyz->gxyz", cas_x, stacked, precision=lax.Precision.HIGH) / NX
    pressure = fields[0]
    grad_x = fields[1]
    grad_y = fields[2]
    grad_z = zdiff(pressure)
    newer = ustar_f - time_step * jnp.stack([grad_x, grad_y, grad_z], axis=0)
    return (newer.astype(jnp.bfloat16)[None], pressure[None])


def solution(mesh):
    return jax.shard_map(
        local,
        mesh=mesh,
        in_specs=(P("sec", None, None, "col", None), P(), P("sec", None), P(), P()),
        out_specs=(P("sec", None, None, "col", None), P("sec", None, "col", None)),
        check_vma=False,
    )
```

```python
import numpy as np
import jax
import jax.numpy as jnp
from jax import lax
from jax.sharding import PartitionSpec as P

NX = 1024
BAND = 32
NB = 10
FR = 32
DISK = 4
KX = 320
SLOTS = 2 * KX


highest = lax.Precision.HIGHEST
time_step = 0.25
screen = 0.01
fringe_rate = 2.0


def slot_modes():
    slots = np.arange(SLOTS)
    return np.where(slots < KX, slots, slots + NX - SLOTS)


def deriv_table():
    index = np.arange(NX)
    offset = (index[:, None] - index[None, :]) % NX
    angle = np.pi * offset / NX
    parity = 1.0 - 2.0 * (offset % 2)
    denom = np.where(offset == 0, 1.0, np.sin(angle))
    table = np.where(offset == 0, 0.0, 0.5 * parity * np.cos(angle) / denom)
    return jnp.asarray(table.astype(np.float32)).astype(jnp.bfloat16)


def cas_table(modes, length):
    cells = np.arange(length)
    angle = 2.0 * np.pi * ((modes[:, None] * cells[None, :]) % length) / length
    return np.cos(angle) + np.sin(angle)


def cosine_np(length):
    index = np.arange(length)
    angle = np.pi * index[:, None] * (2 * index[None, :] + 1) / (2 * length)
    scale = np.where(index == 0, np.sqrt(1.0 / length), np.sqrt(2.0 / length))
    return np.cos(angle) * scale[:, None]


def signed_np(length):
    index = np.arange(length)
    return np.where(index < length // 2, index, np.where(index > length // 2, index - length, 0))


def wave_square(mode_ids, length):
    folded = jnp.minimum(mode_ids, length - mode_ids).astype(jnp.float32)
    return (2.0 * jnp.pi * folded / length) ** 2


def kept_mask(mode_ids, counts):
    folded = jnp.minimum(mode_ids, NX - mode_ids)
    band_of = folded // BAND
    onehot = band_of[:, None] == jnp.arange(NB, dtype=jnp.int32)[None, :]
    limit_per = jnp.sum(jnp.where(onehot, counts[None, :], 0), axis=1)
    return ((folded < KX) & (folded % BAND < limit_per)).astype(jnp.float32)


def zdiff(field):
    zeros = jnp.zeros(field.shape[:-1] + (1,), jnp.float32)
    upper = jnp.concatenate([field[..., 1:], zeros], axis=-1)
    lower = jnp.concatenate([zeros, field[..., :-1]], axis=-1)
    return (upper - lower) * 0.5


def fringe_weights(split_at):
    cells = jnp.arange(NX, dtype=jnp.int32)[:, None]
    plane = jnp.arange(FR, dtype=jnp.int32)[None, :]
    rate = fringe_rate * jnp.sin(jnp.pi * (plane.astype(jnp.float32) + 0.5) / FR) ** 2
    inside = (cells == plane) | (cells == split_at + plane)
    return jnp.where(inside, rate, 0.0)


def turbine_field(cells, thrust, ycoord, count_z, span_total):
    onehot_x = (cells[:, 0][:, None] == jnp.arange(NX, dtype=jnp.int32)[None, :]).astype(
        jnp.float32
    ) * thrust[:, None]
    offset_y = (ycoord[None, :] - cells[:, 1][:, None]) % span_total
    onehot_y = ((offset_y <= DISK) | (offset_y >= span_total - DISK)).astype(jnp.float32)
    offset_z = jnp.abs(jnp.arange(count_z, dtype=jnp.int32)[None, :] - cells[:, 2][:, None])
    onehot_z = (offset_z <= DISK).astype(jnp.float32)
    cross_yz = (onehot_y[:, :, None] * onehot_z[:, None, :]).reshape(cells.shape[0], -1)
    field = jnp.dot(onehot_x.T, cross_yz, precision=lax.Precision.HIGH)
    return field.reshape(NX, ycoord.shape[0], count_z)


def column_solve(columns, local_modes):
    cells_y = columns.shape[1]
    cells_z = columns.shape[2]
    ids_y = np.arange(cells_y)
    cas_y = jnp.asarray(cas_table(ids_y, cells_y).astype(np.float32))
    cos_z = jnp.asarray(cosine_np(cells_z).astype(np.float32))
    wave_y = 2.0 * np.pi * signed_np(cells_y) / cells_y
    back_p = cas_table(ids_y, cells_y) / cells_y
    back_g = wave_y[:, None] * cas_table((-ids_y) % cells_y, cells_y) / cells_y
    back_y = jnp.asarray(np.stack([back_p, back_g]).astype(np.float32))
    first = jnp.einsum("jy,ryz->rjz", cas_y, columns, precision=lax.Precision.HIGH)
    second = jnp.einsum("rjz,mz->rjm", first, cos_z, precision=lax.Precision.HIGH)
    kz_sq = (jnp.pi * jnp.arange(cells_z, dtype=jnp.int32).astype(jnp.float32) / cells_z) ** 2
    eigen = (
        wave_square(local_modes, NX)[:, None, None]
        + wave_square(jnp.arange(cells_y, dtype=jnp.int32), cells_y)[None, :, None]
        + kz_sq[None, None, :]
        + screen
    )
    p_hat = -second / eigen
    back = jnp.einsum("gjy,rjm->rgym", back_y, p_hat, precision=lax.Precision.HIGH)
    return jnp.einsum("rgym,mz->rgyz", back, cos_z, precision=lax.Precision.HIGH)


def halo(block, cols):
    secs = lax.axis_size("sec")
    up = lambda s: [(s * cols + i, s * cols + (i + 1) % cols) for i in range(cols)]
    down = lambda s: [(s * cols + (i + 1) % cols, s * cols + i) for i in range(cols)]
    first = sum([up(s) if s % 2 == 0 else down(s) for s in range(secs)], [])
    second = sum([down(s) if s % 2 == 0 else up(s) for s in range(secs)], [])
    got_first = lax.ppermute(block, ("sec", "col"), first)
    got_second = lax.ppermute(block, ("sec", "col"), second)
    even = lax.axis_index("sec") % 2 == 0
    low = jnp.where(even, got_first, got_second)
    high = jnp.where(even, got_second, got_first)
    return low, high


def local(velocity, thrust, band_counts, farm_split, turbine_cells):
    moving_bf = velocity[0]
    rows_here = moving_bf.shape[2]
    count_z = moving_bf.shape[3]
    col_index = lax.axis_index("col")
    cols = lax.axis_size("col")
    span_total = rows_here * cols
    farm_on = (lax.axis_index("sec") == 1).astype(jnp.float32)
    deriv_bf = deriv_table()
    modes_np = slot_modes()
    cas_x = jnp.asarray(cas_table(modes_np, NX).astype(np.float32))

    low, high = halo(moving_bf, cols)
    moving = moving_bf.astype(jnp.float32)
    along_x = jnp.einsum("ij,cjyz->ciyz", deriv_bf, moving_bf, preferred_element_type=jnp.float32)
    slab, along_x = lax.optimization_barrier((moving_bf[:, NX - FR :], along_x))
    outflow = lax.ppermute(slab, "sec", [(0, 1)])
    along_z = zdiff(moving)
    weights = fringe_weights(farm_split[0]) * farm_on
    target = jnp.einsum("xj,cjyz->cxyz", weights, outflow.astype(jnp.float32), precision=lax.Precision.HIGH)
    fringe = target - jnp.sum(weights, axis=1)[None, :, None, None] * moving
    ycoord = col_index * rows_here + jnp.arange(rows_here, dtype=jnp.int32)
    drag_field = turbine_field(turbine_cells, thrust, ycoord, count_z, span_total) * farm_on
    thrust_force = -0.5 * drag_field * moving[0] * jnp.abs(moving[0])
    local_part = -(moving[0] * along_x + moving[2] * along_z) + fringe
    local_part = jnp.concatenate([local_part[:1] + thrust_force[None], local_part[1:]], axis=0)
    local_part = lax.optimization_barrier(local_part)
    along_y = (high.astype(jnp.float32) - low.astype(jnp.float32)) * 0.5
    tendency = local_part - moving[1] * along_y
    ustar = (moving + time_step * tendency).astype(jnp.bfloat16)
    side_low, side_high = halo(ustar[1], cols)
    ustar_f = ustar.astype(jnp.float32)
    divergence = jnp.einsum("ij,jyz->iyz", deriv_bf, ustar[0], preferred_element_type=jnp.float32)
    divergence = lax.optimization_barrier(divergence + zdiff(ustar_f[2]))
    side_low = side_low.astype(jnp.float32)
    side_high = side_high.astype(jnp.float32)
    divergence = divergence + (side_high - side_low) * 0.5
    source = divergence / time_step
    modes = jnp.asarray(modes_np.astype(np.int32))
    retained = kept_mask(modes, band_counts[0])
    spec = jnp.einsum("kx,xyz->kyz", cas_x, source, precision=lax.Precision.HIGH) * retained[:, None, None]
    columns = lax.all_to_all(spec, "col", split_axis=0, concat_axis=1, tiled=True)
    per_device = columns.shape[0]
    local_modes = lax.dynamic_slice_in_dim(modes, col_index * per_device, per_device)
    solved = column_solve(columns, local_modes)
    back = lax.all_to_all(solved, "col", split_axis=2, concat_axis=0, tiled=True)
    pres_modes = back[:, 0]
    grad_modes = back[:, 1]
    signed = np.where(modes_np < NX // 2, modes_np, modes_np - NX).astype(np.float32)
    mirrored = jnp.concatenate([pres_modes[:1], jnp.flip(pres_modes[1:], axis=0)], axis=0)
    dx_modes = -jnp.asarray(signed)[:, None, None] * mirrored
    stacked = jnp.stack([pres_modes, dx_modes, grad_modes], axis=0)
    fields = jnp.einsum("kx,gkyz->gxyz", cas_x, stacked, precision=lax.Precision.HIGH) / NX
    pressure = fields[0]
    grad_x = fields[1]
    grad_y = fields[2]
    grad_z = zdiff(pressure)
    newer = ustar_f - time_step * jnp.stack([grad_x, grad_y, grad_z], axis=0)
    return (newer.astype(jnp.bfloat16)[None], pressure[None])


def solution(mesh):
    return jax.shard_map(
        local,
        mesh=mesh,
        in_specs=(P("sec", None, None, "col", None), P(), P("sec", None), P(), P()),
        out_specs=(P("sec", None, None, "col", None), P("sec", None, "col", None)),
        check_vma=False,
    )
```
